128 devices in a mesh: user: 16 (over z, x), cand: 8 (over y, core).
Axes of the slice: x: 4, y: 4, z: 4, core: 2. Of those that a mesh axis runs over, the one named last changes fastest.
Arguments:
- cand_emb: bfloat16 [65536, 512], P(('user', 'cand')), may hold values from -40 to 40
- cand_route: int32 [65536], P(('user', 'cand')), may hold values from 0 to 127, as said below
- hist_kv: bfloat16 [2, 16, 1024, 1024], P(None, 'user'), may hold values from -6 to 6
- hist_len: int32 [16], P('user'), may hold values from 256 to 1024, as said below
- w_in: bfloat16 [2, 512, 1024], replicated, may hold values from -0.25 to 0.25
- w_out: bfloat16 [2, 512, 512], replicated, may hold values from -0.25 to 0.25
Outputs:
- scored: float32 [65536, 512], P(('user', 'cand'))
The draws below stay inside these ranges and needn't reach their ends.
Inputs may be any that keep to these rules, and one draw needn't show every extreme that they name: `cand_route`: among the rows of one device no value is named by more than 8 rows, and one and the same value is named by exactly 8 rows on every device. `hist_len`: some user has a full history.
All inputs are finite; a program needn't handle non-finite values.
Results may differ from the reference program's by a relative error of at most 0.003.
Values may be sent and summed in bfloat16 or wider, within the bound.
No kernel may reach another device: no remote copies, remote signals or barrier semaphores. Data moves between devices by JAX's collectives and lax.ppermute only.
A program may use at most 64 MiB of HBM per device.

```python
import jax
import jax.numpy as jnp
from jax import lax

D = 512
HEADS = 4
LAYERS = 2
HIST = 1024
R_DEV = 512
SCORERS = 128
USERS = 16
CAP = 8
CANDS = 65536
N_CAND = 8


def draw_cand_route(key, part):
    hot_scorer = jax.random.randint(jax.random.fold_in(key, 7), (), 0, SCORERS).astype(jnp.int32)
    repeated = jnp.arange((SCORERS - 1) * CAP, dtype=jnp.int32) // CAP
    others = jnp.where(repeated >= hot_scorer, repeated + 1, repeated).astype(jnp.int32)

    def one_device(device_index):
        block_key = jax.random.fold_in(key, device_index + 11)
        picked = jax.random.permutation(block_key, others)[:R_DEV - CAP]
        device_rows = jnp.concatenate([jnp.full((CAP,), hot_scorer, jnp.int32), picked])
        return jax.random.permutation(jax.random.fold_in(block_key, 3), device_rows)
    return jax.vmap(one_device)(jnp.arange(SCORERS, dtype=jnp.int32)).reshape(-1).astype(jnp.int32)


def draw_hist_len(key, part):
    lengths = jax.random.randint(key, (USERS,), HIST // 4, HIST + 1).astype(jnp.int32)
    full_user = jax.random.randint(jax.random.fold_in(key, 5), (), 0, USERS)
    return lengths.at[full_user].set(HIST).astype(jnp.int32)


def draw_cand_emb(key, part):
    entry_key = jax.random.fold_in(key, 21)
    row_key = jax.random.fold_in(key, 22)
    column_key = jax.random.fold_in(key, 23)
    entries = jnp.clip(jax.random.normal(entry_key, (CANDS, D), jnp.float32), -4.0, 4.0)
    row_scale = jnp.exp(jax.random.uniform(row_key, (CANDS, 1), jnp.float32, -1.15, 1.15))
    column_scale = jnp.exp(jax.random.uniform(column_key, (1, D), jnp.float32, -1.15, 1.15))
    return (entries * row_scale * column_scale).astype(jnp.bfloat16)


def level_of(rng, extent, pieces, least, top_value):
    def one(position, shards_of):
        steps = jax.random.uniform(jax.random.fold_in(jax.random.fold_in(rng, 6), position), (shards_of,), jnp.float32, least / len(pieces), top_value / len(pieces))
        return jnp.repeat(jnp.exp(steps), extent[position] // shards_of).reshape((-1,) + (1,) * (len(extent) - position - 1))

    factor_of = one(*pieces[0])
    for cut in pieces[1:]:
        factor_of = factor_of * one(*cut)
    return factor_of


def gaussian(stream_key, dims, deviation, most, pieces=(), kind=jnp.bfloat16):
    array = jax.random.normal(stream_key, dims, jnp.float32) * deviation
    if len(pieces) > 0:
        array = level_of(stream_key, dims, pieces, -0.22, 0.18) * array
    return jnp.clip(array, min=-most, max=most).astype(kind)


def setup_inputs(seed: int = 0) -> dict:
    key_list = jax.random.split(jax.random.key(seed), 7)
    return {
        "cand_emb": draw_cand_emb(jax.random.fold_in(key_list[6], 71), 0),
        "cand_route": draw_cand_route(jax.random.fold_in(key_list[6], 71), 0),
        "hist_kv": gaussian(key_list[2], (LAYERS, USERS, HIST, 2 * D), 1.0, 6.0, ((1, 16),)),
        "hist_len": draw_hist_len(jax.random.fold_in(key_list[6], 71), 0),
        "w_in": gaussian(key_list[4], (LAYERS, D, 2 * D), D ** -0.5, 0.25),
        "w_out": gaussian(key_list[5], (LAYERS, D, D), D ** -0.5, 0.25),
    }


epsilon = 1e-05

def layer_normed(values):
    center = values - lax.optimization_barrier(jnp.mean(values, axis=-1, keepdims=True))
    spread = lax.optimization_barrier(jnp.mean(center * center, axis=-1, keepdims=True))
    return center * lax.rsqrt(spread + epsilon)

def run_layers(cand_rows, history, length, w_in, w_out):
    row_count, features = cand_rows.shape
    head_dim = features // HEADS
    factor = head_dim ** (-0.5)
    in_history = jnp.arange(HIST, dtype=jnp.int32) < length
    residual = cand_rows.astype(jnp.float32)
    for layer_index in range(LAYERS):
        normed = layer_normed(residual).astype(jnp.bfloat16)
        projected = jax.nn.silu(jnp.dot(normed, w_in[layer_index], preferred_element_type=jnp.float32)).astype(jnp.bfloat16)
        projected = lax.optimization_barrier(projected).astype(jnp.float32)
        queries = projected[:, features:].reshape(row_count, HEADS, head_dim)
        hist_keys = history[layer_index, :, :features].astype(jnp.float32).reshape(HIST, HEADS, head_dim)
        hist_values = history[layer_index, :, features:].astype(jnp.float32).reshape(HIST, HEADS, head_dim)
        scores = jnp.einsum('bhd,jhd->hbj', queries, hist_keys)
        weight = jnp.where(in_history[None, None, :], jax.nn.silu(scores * factor), 0.0).astype(jnp.bfloat16)
        weight = lax.optimization_barrier(weight).astype(jnp.float32)
        attended = jnp.einsum('hbj,jhd->bhd', weight, hist_values).reshape(row_count, features)
        branch = (layer_normed(attended) * projected[:, :features]).astype(jnp.bfloat16)
        residual = residual + jnp.dot(branch, w_out[layer_index], preferred_element_type=jnp.float32)
    return residual

def reference(cand_emb, cand_route, hist_kv, hist_len, w_in, w_out):
    ordering = jnp.argsort(cand_route, stable=True).astype(jnp.int32)
    sorted_rows = cand_emb[ordering]
    counts = jax.ops.segment_sum(jnp.ones_like(cand_route), cand_route, SCORERS).astype(jnp.int32)
    offsets = (jnp.cumsum(counts) - counts).astype(jnp.int32)
    window = SCORERS * CAP
    padded = jnp.concatenate([sorted_rows, jnp.zeros((window, D), cand_emb.dtype)], axis=0)

    def per_scorer(results, scorer):
        start_row = offsets[scorer].astype(jnp.int32)
        block_rows = lax.dynamic_slice_in_dim(padded, start_row, window, 0)
        owner_user = scorer // N_CAND
        finished = run_layers(block_rows, hist_kv[:, owner_user], hist_len[owner_user], w_in, w_out)
        return (lax.dynamic_update_slice_in_dim(results, finished, start_row, 0), None)
    results, unused = lax.scan(per_scorer, jnp.zeros((CANDS + window, D), jnp.float32), jnp.arange(SCORERS, dtype=jnp.int32))
    return jnp.zeros((CANDS, D), jnp.float32).at[ordering].set(results[:CANDS])
```

```python
import functools

import jax
import jax.numpy as jnp
from jax import lax
from jax.experimental import pallas as pl
from jax.experimental.pallas import tpu as pltpu
from jax.sharding import PartitionSpec as P

HEADS = 4
ROW_BLOCK = 256

epsilon = 1e-05


def half_silu(t):
    return t + t * jnp.tanh(t)


def layer_normed(values):
    center = values - jnp.mean(values, axis=-1, keepdims=True)
    spread = jnp.mean(center * center, axis=-1, keepdims=True)
    return center * lax.rsqrt(spread + epsilon)


def layers_kernel(length_ref, rows_ref, hist_ref, w_in_ref, w_out_ref, out_ref):
    block_rows, features = rows_ref.shape
    layer_count = w_in_ref.shape[0]
    history_span = hist_ref.shape[1]
    head_dim = features // HEADS
    factor = head_dim ** (-0.5)
    length = length_ref[0]
    in_history = lax.broadcasted_iota(jnp.int32, (1, history_span), 1) < length

    start = rows_ref[...].astype(jnp.float32)
    residual = start
    for layer_index in range(layer_count):
        normed = layer_normed(residual).astype(jnp.bfloat16)
        mixed = jnp.dot(normed, w_in_ref[layer_index], preferred_element_type=jnp.float32)
        projected = half_silu(mixed * 0.5).astype(jnp.bfloat16)
        gate = projected[:, :features].astype(jnp.float32)
        heads = []
        for head in range(HEADS):
            low = head * head_dim
            query = projected[:, features + low:features + low + head_dim]
            keys = hist_ref[layer_index, :, low:low + head_dim]
            values = hist_ref[layer_index, :, features + low:features + low + head_dim]
            scores = lax.dot_general(
                query, keys, (((1,), (1,)), ((), ())), preferred_element_type=jnp.float32
            )
            weight = half_silu(scores * (0.5 * factor))
            weight = jnp.where(in_history, weight, 0.0).astype(jnp.bfloat16)
            heads.append(jnp.dot(weight, values, preferred_element_type=jnp.float32))
        attended = jnp.concatenate(heads, axis=1)
        branch = (layer_normed(attended) * gate).astype(jnp.bfloat16)
        residual = residual + jnp.dot(
            branch, w_out_ref[layer_index], preferred_element_type=jnp.float32
        )
    out_ref[...] = (residual - start).astype(out_ref.dtype)


def run_layers(rows, history, length, w_in, w_out):
    row_count, features = rows.shape
    layer_count, history_span, width = history.shape
    grid_spec = pltpu.PrefetchScalarGridSpec(
        num_scalar_prefetch=1,
        grid=(row_count // ROW_BLOCK,),
        in_specs=[
            pl.BlockSpec((ROW_BLOCK, features), lambda i, n: (i, 0)),
            pl.BlockSpec((layer_count, history_span, width), lambda i, n: (0, 0, 0)),
            pl.BlockSpec(w_in.shape, lambda i, n: (0, 0, 0)),
            pl.BlockSpec(w_out.shape, lambda i, n: (0, 0, 0)),
        ],
        out_specs=pl.BlockSpec((ROW_BLOCK, features), lambda i, n: (i, 0)),
    )
    flops = 2 * row_count * layer_count * (
        features * 2 * features + 2 * history_span * features + features * features
    )
    return pl.pallas_call(
        layers_kernel,
        grid_spec=grid_spec,
        out_shape=jax.ShapeDtypeStruct((row_count, features), jnp.bfloat16),
        compiler_params=pltpu.CompilerParams(
            dimension_semantics=("arbitrary",), vmem_limit_bytes=48 * 1024 * 1024
        ),
        cost_estimate=pl.CostEstimate(
            flops=flops,
            transcendentals=row_count * layer_count * (HEADS * history_span + 2 * features),
            bytes_accessed=2 * (history.size + w_in.size + w_out.size + 2 * rows.size),
        ),
    )(length, rows, history, w_in, w_out)


def local(cand_emb, cand_route, hist_kv, hist_len, w_in, w_out):
    cand_rows, features = cand_emb.shape
    user_count = lax.axis_size("user")
    group_size = lax.axis_size("cand")
    scorers = user_count * group_size
    capacity = 2 * cand_rows // scorers
    slots = scorers * capacity
    onehot = (cand_route[:, None] == jnp.arange(scorers, dtype=jnp.int32)[None, :]).astype(
        jnp.int32
    )
    ranking = jnp.sum(jnp.cumsum(onehot, axis=0) * onehot, axis=1) - 1
    position = cand_route * capacity + ranking
    placing = (
        lax.broadcasted_iota(jnp.int32, (slots, cand_rows), 0) == position[None, :]
    ).astype(jnp.bfloat16)
    packed = jnp.dot(placing, cand_emb, preferred_element_type=jnp.float32).astype(jnp.bfloat16)
    outgoing = packed.reshape(scorers, capacity, features)
    items = lax.all_to_all(outgoing, ("user", "cand"), split_axis=0, concat_axis=0, tiled=True)
    history = hist_kv.reshape(hist_kv.shape[0], hist_kv.shape[2], hist_kv.shape[3])
    delta = run_layers(items.reshape(-1, features), history, hist_len, w_in, w_out)
    returned = lax.all_to_all(
        delta.reshape(items.shape), ("user", "cand"), split_axis=0, concat_axis=0, tiled=True
    )
    gathered = lax.dot_general(
        placing,
        returned.reshape(-1, features),
        (((0,), (0,)), ((), ())),
        preferred_element_type=jnp.float32,
    )
    return cand_emb.astype(jnp.float32) + gathered


def solution(mesh):
    placed = (
        P(("user", "cand"), None),
        P(("user", "cand")),
        P(None, "user", None, None),
        P("user"),
        P(),
        P(),
    )
    return jax.shard_map(
        local, mesh=mesh, in_specs=placed, out_specs=P(("user", "cand"), None), check_vma=False
    )
```

```python
import jax
import jax.numpy as jnp
from jax import lax
from jax.experimental import pallas as pl
from jax.experimental.pallas import tpu as pltpu
from jax.sharding import PartitionSpec as P

HEADS = 4
SLOT_BLOCK = 16

epsilon = 1e-05


def half_silu(t):
    return t + t * jnp.tanh(t)


def layer_normed(values):
    center = values - jnp.mean(values, axis=-1, keepdims=True)
    spread = jnp.mean(center * center, axis=-1, keepdims=True)
    return center * lax.rsqrt(spread + epsilon)


def layers_kernel(length_ref, busy_ref, rows_ref, hist_ref, w_in_ref, w_out_ref, out_ref):
    sources, slots, features = rows_ref.shape
    block_rows = sources * slots
    layer_count = w_in_ref.shape[0]
    history_span = hist_ref.shape[1]
    head_dim = features // HEADS
    factor = head_dim ** (-0.5)
    step = pl.program_id(0)

    @pl.when(busy_ref[step] == 0)
    def _():
        out_ref[...] = jnp.zeros(out_ref.shape, out_ref.dtype)

    @pl.when(busy_ref[step] != 0)
    def _():
        length = length_ref[0]
        in_history = lax.broadcasted_iota(jnp.int32, (history_span, 1), 0) < length
        start = rows_ref[...].astype(jnp.float32).reshape(block_rows, features)
        residual = start
        for layer_index in range(layer_count):
            normed = layer_normed(residual).astype(jnp.bfloat16)
            mixed = jnp.dot(normed, w_in_ref[layer_index], preferred_element_type=jnp.float32)
            projected = half_silu(mixed * 0.5).astype(jnp.bfloat16)
            gate = projected[:, :features].astype(jnp.float32)
            values_all = jnp.where(
                in_history, hist_ref[layer_index, :, features:], jnp.zeros((), jnp.bfloat16)
            )
            heads = []
            for head in range(HEADS):
                low = head * head_dim
                query = projected[:, features + low:features + low + head_dim]
                keys = hist_ref[layer_index, :, low:low + head_dim]
                scores = lax.dot_general(
                    query, keys, (((1,), (1,)), ((), ())), preferred_element_type=jnp.float32
                )
                weight = half_silu(scores * (0.5 * factor)).astype(jnp.bfloat16)
                heads.append(
                    jnp.dot(
                        weight,
                        values_all[:, low:low + head_dim],
                        preferred_element_type=jnp.float32,
                    )
                )
            attended = jnp.concatenate(heads, axis=1)
            branch = (layer_normed(attended) * gate).astype(jnp.bfloat16)
            residual = residual + jnp.dot(
                branch, w_out_ref[layer_index], preferred_element_type=jnp.float32
            )
        out_ref[...] = (residual - start).reshape(sources, slots, features).astype(out_ref.dtype)


def run_layers(buckets, history, length, w_in, w_out):
    sources, capacity, features = buckets.shape
    layer_count, history_span, width = history.shape
    steps = capacity // SLOT_BLOCK
    busy = jnp.any(
        buckets.reshape(sources, steps, SLOT_BLOCK * features) != 0, axis=(0, 2)
    ).astype(jnp.int32)
    grid_spec = pltpu.PrefetchScalarGridSpec(
        num_scalar_prefetch=2,
        grid=(steps,),
        in_specs=[
            pl.BlockSpec((sources, SLOT_BLOCK, features), lambda i, n, b: (0, i, 0)),
            pl.BlockSpec((layer_count, history_span, width), lambda i, n, b: (0, 0, 0)),
            pl.BlockSpec(w_in.shape, lambda i, n, b: (0, 0, 0)),
            pl.BlockSpec(w_out.shape, lambda i, n, b: (0, 0, 0)),
        ],
        out_specs=pl.BlockSpec((sources, SLOT_BLOCK, features), lambda i, n, b: (0, i, 0)),
    )
    row_count = sources * capacity
    flops = 2 * row_count * layer_count * (
        features * 2 * features + 2 * history_span * features + features * features
    )
    return pl.pallas_call(
        layers_kernel,
        grid_spec=grid_spec,
        out_shape=jax.ShapeDtypeStruct(buckets.shape, jnp.bfloat16),
        compiler_params=pltpu.CompilerParams(
            dimension_semantics=("arbitrary",), vmem_limit_bytes=48 * 1024 * 1024
        ),
        cost_estimate=pl.CostEstimate(
            flops=flops,
            transcendentals=row_count * layer_count * (HEADS * history_span + 2 * features),
            bytes_accessed=2 * (history.size + w_in.size + w_out.size + 2 * buckets.size),
        ),
    )(length, busy, buckets, history, w_in, w_out)


def local(cand_emb, cand_route, hist_kv, hist_len, w_in, w_out):
    cand_rows, features = cand_emb.shape
    user_count = lax.axis_size("user")
    group_size = lax.axis_size("cand")
    capacity = 2 * cand_rows // user_count
    slots = user_count * capacity
    owner = cand_route // group_size
    onehot = (owner[:, None] == jnp.arange(user_count, dtype=jnp.int32)[None, :]).astype(
        jnp.int32
    )
    ranking = jnp.sum(jnp.cumsum(onehot, axis=0) * onehot, axis=1) - 1
    position = owner * capacity + ranking
    placing = (
        lax.broadcasted_iota(jnp.int32, (slots, cand_rows), 0) == position[None, :]
    ).astype(jnp.bfloat16)
    packed = jnp.dot(placing, cand_emb, preferred_element_type=jnp.float32).astype(jnp.bfloat16)
    outgoing = packed.reshape(user_count, capacity, features)
    items = lax.all_to_all(outgoing, "user", split_axis=0, concat_axis=0, tiled=True)
    history = hist_kv.reshape(hist_kv.shape[0], hist_kv.shape[2], hist_kv.shape[3])
    delta = run_layers(items, history, hist_len, w_in, w_out)
    returned = lax.all_to_all(delta, "user", split_axis=0, concat_axis=0, tiled=True)
    gathered = lax.dot_general(
        placing,
        returned.reshape(-1, features),
        (((0,), (0,)), ((), ())),
        preferred_element_type=jnp.float32,
    )
    return cand_emb.astype(jnp.float32) + gathered


def solution(mesh):
    placed = (
        P(("user", "cand"), None),
        P(("user", "cand")),
        P(None, "user", None, None),
        P("user"),
        P(),
        P(),
    )
    return jax.shard_map(
        local, mesh=mesh, in_specs=placed, out_specs=P(("user", "cand"), None), check_vma=False
    )
```

```python
import functools

import jax
import jax.numpy as jnp
from jax import lax
from jax.experimental import pallas as pl
from jax.experimental.pallas import tpu as pltpu
from jax.sharding import PartitionSpec as P

HEADS = 4
SLOT_BLOCK = 16

epsilon = 1e-05


def silu(v):
    return v * jax.nn.sigmoid(v)


def layer_normed(values):
    center = values - jnp.mean(values, axis=-1, keepdims=True)
    spread = jnp.mean(center * center, axis=-1, keepdims=True)
    return center * lax.rsqrt(spread + epsilon)


def layers_kernel(length_ref, busy_ref, rows_ref, hist_ref, w_in_ref, w_out_ref, out_ref):
    sources, slots, features = rows_ref.shape
    block_rows = sources * slots
    layer_count = w_in_ref.shape[0]
    history_span = hist_ref.shape[1]
    head_dim = features // HEADS
    factor = head_dim ** (-0.5)
    step = pl.program_id(0)

    @pl.when(busy_ref[step] == 0)
    def _():
        out_ref[...] = jnp.zeros(out_ref.shape, out_ref.dtype)

    @pl.when(busy_ref[step] != 0)
    def _():
        length = length_ref[0]
        in_history = lax.broadcasted_iota(jnp.int32, (history_span, 1), 0) < length
        start = rows_ref[...].astype(jnp.float32).reshape(block_rows, features)
        residual = start
        for layer_index in range(layer_count):
            normed = layer_normed(residual).astype(jnp.bfloat16)
            mixed = jnp.dot(normed, w_in_ref[layer_index], preferred_element_type=jnp.float32)
            projected = silu(mixed).astype(jnp.bfloat16)
            gate = projected[:, :features].astype(jnp.float32)
            values_all = jnp.where(
                in_history, hist_ref[layer_index, :, features:], jnp.zeros((), jnp.bfloat16)
            )
            heads = []
            for head in range(HEADS):
                low = head * head_dim
                query = projected[:, features + low:features + low + head_dim]
                query = (query.astype(jnp.float32) * factor).astype(jnp.bfloat16)
                keys = hist_ref[layer_index, :, low:low + head_dim]
                scores = lax.dot_general(
                    query, keys, (((1,), (1,)), ((), ())), preferred_element_type=jnp.float32
                )
                weight = silu(scores).astype(jnp.bfloat16)
                heads.append(
                    jnp.dot(
                        weight,
                        values_all[:, low:low + head_dim],
                        preferred_element_type=jnp.float32,
                    )
                )
            attended = jnp.concatenate(heads, axis=1)
            branch = (layer_normed(attended) * gate).astype(jnp.bfloat16)
            residual = residual + jnp.dot(
                branch, w_out_ref[layer_index], preferred_element_type=jnp.float32
            )
        out_ref[...] = (residual - start).reshape(sources, slots, features).astype(out_ref.dtype)


def run_layers(buckets, history, length, w_in, w_out):
    sources, capacity, features = buckets.shape
    layer_count, history_span, width = history.shape
    steps = capacity // SLOT_BLOCK
    busy = jnp.any(
        buckets.reshape(sources, steps, SLOT_BLOCK * features) != 0, axis=(0, 2)
    ).astype(jnp.int32)
    grid_spec = pltpu.PrefetchScalarGridSpec(
        num_scalar_prefetch=2,
        grid=(steps,),
        in_specs=[
            pl.BlockSpec((sources, SLOT_BLOCK, features), lambda i, n, b: (0, i, 0)),
            pl.BlockSpec((layer_count, history_span, width), lambda i, n, b: (0, 0, 0)),
            pl.BlockSpec(w_in.shape, lambda i, n, b: (0, 0, 0)),
            pl.BlockSpec(w_out.shape, lambda i, n, b: (0, 0, 0)),
        ],
        out_specs=pl.BlockSpec((sources, SLOT_BLOCK, features), lambda i, n, b: (0, i, 0)),
    )
    row_count = sources * capacity
    flops = 2 * row_count * layer_count * (
        features * 2 * features + 2 * history_span * features + features * features
    )
    return pl.pallas_call(
        layers_kernel,
        grid_spec=grid_spec,
        out_shape=jax.ShapeDtypeStruct(buckets.shape, jnp.bfloat16),
        compiler_params=pltpu.CompilerParams(
            dimension_semantics=("arbitrary",), vmem_limit_bytes=48 * 1024 * 1024
        ),
        cost_estimate=pl.CostEstimate(
            flops=flops,
            transcendentals=row_count * layer_count * (HEADS * history_span + 2 * features),
            bytes_accessed=2 * (history.size + w_in.size + w_out.size + 2 * buckets.size),
        ),
    )(length, busy, buckets, history, w_in, w_out)


def pack_kernel(route_ref, emb_ref, packed_ref, position_ref, *, group_size, user_count):
    cand_rows = emb_ref.shape[0]
    capacity = packed_ref.shape[0] // user_count
    owner = route_ref[...] // group_size
    member = (lax.broadcasted_iota(jnp.int32, (user_count, cand_rows), 0) == owner).astype(
        jnp.float32
    )
    earlier = (
        lax.broadcasted_iota(jnp.int32, (cand_rows, cand_rows), 0)
        < lax.broadcasted_iota(jnp.int32, (cand_rows, cand_rows), 1)
    ).astype(jnp.bfloat16)
    before = jnp.dot(member.astype(jnp.bfloat16), earlier, preferred_element_type=jnp.float32)
    ranking = jnp.sum(member * before, axis=0, keepdims=True).astype(jnp.int32)
    position = owner * capacity + ranking
    position_ref[...] = position
    placing = (
        lax.broadcasted_iota(jnp.int32, (packed_ref.shape[0], cand_rows), 0) == position
    ).astype(jnp.bfloat16)
    packed_ref[...] = jnp.dot(
        placing, emb_ref[...], preferred_element_type=jnp.float32
    ).astype(packed_ref.dtype)


def pack_rows(cand_emb, cand_route, user_count, group_size):
    cand_rows, features = cand_emb.shape
    slots = 2 * cand_rows
    return pl.pallas_call(
        functools.partial(pack_kernel, group_size=group_size, user_count=user_count),
        out_shape=(
            jax.ShapeDtypeStruct((slots, features), jnp.bfloat16),
            jax.ShapeDtypeStruct((1, cand_rows), jnp.int32),
        ),
        in_specs=[pl.BlockSpec(memory_space=pltpu.VMEM)] * 2,
        out_specs=(pl.BlockSpec(memory_space=pltpu.VMEM),) * 2,
        cost_estimate=pl.CostEstimate(
            flops=2 * slots * cand_rows * features + 2 * user_count * cand_rows * cand_rows,
            transcendentals=0,
            bytes_accessed=2 * (cand_emb.size + slots * features),
        ),
    )(cand_route.reshape(1, cand_rows), cand_emb)


def local(cand_emb, cand_route, hist_kv, hist_len, w_in, w_out):
    cand_rows, features = cand_emb.shape
    user_count = lax.axis_size("user")
    group_size = lax.axis_size("cand")
    packed, position = pack_rows(cand_emb, cand_route, user_count, group_size)
    slots = packed.shape[0]
    capacity = slots // user_count
    placing = (lax.broadcasted_iota(jnp.int32, (slots, cand_rows), 0) == position).astype(
        jnp.bfloat16
    )
    outgoing = packed.reshape(user_count, capacity, features)
    items = lax.all_to_all(outgoing, "user", split_axis=0, concat_axis=0, tiled=True)
    history = hist_kv.reshape(hist_kv.shape[0], hist_kv.shape[2], hist_kv.shape[3])
    delta = run_layers(items, history, hist_len, w_in, w_out)
    returned = lax.all_to_all(delta, "user", split_axis=0, concat_axis=0, tiled=True)
    gathered = lax.dot_general(
        placing,
        returned.reshape(-1, features),
        (((0,), (0,)), ((), ())),
        preferred_element_type=jnp.float32,
    )
    return cand_emb.astype(jnp.float32) + gathered


def solution(mesh):
    placed = (
        P(("user", "cand"), None),
        P(("user", "cand")),
        P(None, "user", None, None),
        P("user"),
        P(),
        P(),
    )
    return jax.shard_map(
        local, mesh=mesh, in_specs=placed, out_specs=P(("user", "cand"), None), check_vma=False
    )
```

```python
import functools

import jax
import jax.numpy as jnp
from jax import lax
from jax.experimental import pallas as pl
from jax.experimental.pallas import tpu as pltpu
from jax.sharding import PartitionSpec as P

HEADS = 4
SLOT_BLOCK = 16

epsilon = 1e-05


def silu(v):
    return v * jax.nn.sigmoid(v)


def layer_normed(values):
    center = values - jnp.mean(values, axis=-1, keepdims=True)
    spread = jnp.mean(center * center, axis=-1, keepdims=True)
    return center * lax.rsqrt(spread + epsilon)


def layers_kernel(length_ref, busy_ref, rows_ref, hist_ref, w_in_ref, w_out_ref, out_ref):
    sources, slots, features = rows_ref.shape
    block_rows = sources * slots
    layer_count = w_in_ref.shape[0]
    history_span = hist_ref.shape[1]
    head_dim = features // HEADS
    factor = head_dim ** (-0.5)
    step = pl.program_id(0)

    @pl.when(busy_ref[step] == 0)
    def _():
        out_ref[...] = jnp.zeros(out_ref.shape, out_ref.dtype)

    @pl.when(busy_ref[step] != 0)
    def _():
        length = length_ref[0]
        in_history = lax.broadcasted_iota(jnp.int32, (history_span, 1), 0) < length
        start = rows_ref[...].astype(jnp.float32).reshape(block_rows, features)
        residual = start
        for layer_index in range(layer_count):
            normed = layer_normed(residual).astype(jnp.bfloat16)
            mixed = jnp.dot(normed, w_in_ref[layer_index], preferred_element_type=jnp.float32)
            projected = silu(mixed).astype(jnp.bfloat16)
            gate = projected[:, :features].astype(jnp.float32)
            values_all = jnp.where(
                in_history, hist_ref[layer_index, :, features:], jnp.zeros((), jnp.bfloat16)
            )
            heads = []
            for head in range(HEADS):
                low = head * head_dim
                query = projected[:, features + low:features + low + head_dim]
                keys = hist_ref[layer_index, :, low:low + head_dim]
                scores = lax.dot_general(
                    query, keys, (((1,), (1,)), ((), ())), preferred_element_type=jnp.float32
                )
                weight = silu(scores * factor).astype(jnp.bfloat16)
                heads.append(
                    jnp.dot(
                        weight,
                        values_all[:, low:low + head_dim],
                        preferred_element_type=jnp.float32,
                    )
                )
            attended = jnp.concatenate(heads, axis=1)
            branch = (layer_normed(attended) * gate).astype(jnp.bfloat16)
            residual = residual + jnp.dot(
                branch, w_out_ref[layer_index], preferred_element_type=jnp.float32
            )
        out_ref[...] = (residual - start).reshape(sources, slots, features).astype(out_ref.dtype)


def run_layers(buckets, history, length, w_in, w_out):
    sources, capacity, features = buckets.shape
    layer_count, history_span, width = history.shape
    steps = capacity // SLOT_BLOCK
    busy = jnp.any(
        buckets.reshape(sources, steps, SLOT_BLOCK * features) != 0, axis=(0, 2)
    ).astype(jnp.int32)
    grid_spec = pltpu.PrefetchScalarGridSpec(
        num_scalar_prefetch=2,
        grid=(steps,),
        in_specs=[
            pl.BlockSpec((sources, SLOT_BLOCK, features), lambda i, n, b: (0, i, 0)),
            pl.BlockSpec((layer_count, history_span, width), lambda i, n, b: (0, 0, 0)),
            pl.BlockSpec(w_in.shape, lambda i, n, b: (0, 0, 0)),
            pl.BlockSpec(w_out.shape, lambda i, n, b: (0, 0, 0)),
        ],
        out_specs=pl.BlockSpec((sources, SLOT_BLOCK, features), lambda i, n, b: (0, i, 0)),
    )
    row_count = sources * capacity
    flops = 2 * row_count * layer_count * (
        features * 2 * features + 2 * history_span * features + features * features
    )
    return pl.pallas_call(
        layers_kernel,
        grid_spec=grid_spec,
        out_shape=jax.ShapeDtypeStruct(buckets.shape, jnp.bfloat16),
        compiler_params=pltpu.CompilerParams(
            dimension_semantics=("arbitrary",), vmem_limit_bytes=48 * 1024 * 1024
        ),
        cost_estimate=pl.CostEstimate(
            flops=flops,
            transcendentals=row_count * layer_count * (HEADS * history_span + 2 * features),
            bytes_accessed=2 * (history.size + w_in.size + w_out.size + 2 * buckets.size),
        ),
    )(length, busy, buckets, history, w_in, w_out)


def pack_kernel(route_ref, emb_ref, packed_ref, position_ref, *, group_size, user_count):
    cand_rows = emb_ref.shape[0]
    capacity = packed_ref.shape[0] // user_count
    owner = route_ref[...] // group_size
    member = (lax.broadcasted_iota(jnp.int32, (user_count, cand_rows), 0) == owner).astype(
        jnp.float32
    )
    earlier = (
        lax.broadcasted_iota(jnp.int32, (cand_rows, cand_rows), 0)
        < lax.broadcasted_iota(jnp.int32, (cand_rows, cand_rows), 1)
    ).astype(jnp.bfloat16)
    before = jnp.dot(member.astype(jnp.bfloat16), earlier, preferred_element_type=jnp.float32)
    ranking = jnp.sum(member * before, axis=0, keepdims=True).astype(jnp.int32)
    position = owner * capacity + ranking
    position_ref[...] = position
    placing = (
        lax.broadcasted_iota(jnp.int32, (packed_ref.shape[0], cand_rows), 0) == position
    ).astype(jnp.bfloat16)
    packed_ref[...] = jnp.dot(
        placing, emb_ref[...], preferred_element_type=jnp.float32
    ).astype(packed_ref.dtype)


def pack_rows(cand_emb, cand_route, user_count, group_size):
    cand_rows, features = cand_emb.shape
    slots = 2 * cand_rows
    return pl.pallas_call(
        functools.partial(pack_kernel, group_size=group_size, user_count=user_count),
        out_shape=(
            jax.ShapeDtypeStruct((slots, features), jnp.bfloat16),
            jax.ShapeDtypeStruct((1, cand_rows), jnp.int32),
        ),
        in_specs=[pl.BlockSpec(memory_space=pltpu.VMEM)] * 2,
        out_specs=(pl.BlockSpec(memory_space=pltpu.VMEM),) * 2,
        cost_estimate=pl.CostEstimate(
            flops=2 * slots * cand_rows * features + 2 * user_count * cand_rows * cand_rows,
            transcendentals=0,
            bytes_accessed=2 * (cand_emb.size + slots * features),
        ),
    )(cand_route.reshape(1, cand_rows), cand_emb)


def local(cand_emb, cand_route, hist_kv, hist_len, w_in, w_out):
    cand_rows, features = cand_emb.shape
    user_count = lax.axis_size("user")
    group_size = lax.axis_size("cand")
    packed, position = pack_rows(cand_emb, cand_route, user_count, group_size)
    slots = packed.shape[0]
    capacity = slots // user_count
    placing = (lax.broadcasted_iota(jnp.int32, (slots, cand_rows), 0) == position).astype(
        jnp.bfloat16
    )
    outgoing = packed.reshape(user_count, capacity, features)
    items = lax.all_to_all(outgoing, "user", split_axis=0, concat_axis=0, tiled=True)
    history = hist_kv.reshape(hist_kv.shape[0], hist_kv.shape[2], hist_kv.shape[3])
    delta = run_layers(items, history, hist_len, w_in, w_out)
    returned = lax.all_to_all(delta, "user", split_axis=0, concat_axis=0, tiled=True)
    gathered = lax.dot_general(
        placing,
        returned.reshape(-1, features),
        (((0,), (0,)), ((), ())),
        preferred_element_type=jnp.float32,
    )
    return cand_emb.astype(jnp.float32) + gathered


def solution(mesh):
    placed = (
        P(("user", "cand"), None),
        P(("user", "cand")),
        P(None, "user", None, None),
        P("user"),
        P(),
        P(),
    )
    return jax.shard_map(
        local, mesh=mesh, in_specs=placed, out_specs=P(("user", "cand"), None), check_vma=False
    )
```

```python
import functools

import jax
import jax.numpy as jnp
from jax import lax
from jax.experimental import pallas as pl
from jax.experimental.pallas import tpu as pltpu
from jax.sharding import PartitionSpec as P

HEADS = 4
SLOT_BLOCK = 16

epsilon = 1e-05


def silu(v):
    return v * jax.nn.sigmoid(v)


def layer_normed(values):
    center = values - jnp.mean(values, axis=-1, keepdims=True)
    spread = jnp.mean(center * center, axis=-1, keepdims=True)
    return center * lax.rsqrt(spread + epsilon)


def layers_kernel(
    length_ref, busy_ref, rows_ref, w_in_ref, hist_hbm, w_out_hbm, out_ref, hist_ref, w_out_ref,
    copy_sems,
):
    sources, slots, features = rows_ref.shape
    block_rows = sources * slots
    layer_count = w_in_ref.shape[0]
    history_span = hist_ref.shape[1]
    head_dim = features // HEADS
    factor = head_dim ** (-0.5)
    step = pl.program_id(0)
    copies = [
        pltpu.make_async_copy(hist_hbm.at[layer], hist_ref.at[layer], copy_sems.at[layer])
        for layer in range(layer_count)
    ]
    copies.append(pltpu.make_async_copy(w_out_hbm, w_out_ref, copy_sems.at[layer_count]))

    @pl.when(step == 0)
    def _():
        for copy in copies:
            copy.start()

    def arrive(index):
        @pl.when(step == 0)
        def _():
            copies[index].wait()

    @pl.when(busy_ref[step] == 0)
    def _():
        out_ref[...] = jnp.zeros(out_ref.shape, out_ref.dtype)
        for index in range(len(copies)):
            arrive(index)

    @pl.when(busy_ref[step] != 0)
    def _():
        length = length_ref[0]
        in_history = lax.broadcasted_iota(jnp.int32, (history_span, 1), 0) < length
        start = rows_ref[...].astype(jnp.float32).reshape(block_rows, features)
        residual = start
        for layer_index in range(layer_count):
            normed = layer_normed(residual).astype(jnp.bfloat16)
            mixed = jnp.dot(normed, w_in_ref[layer_index], preferred_element_type=jnp.float32)
            projected = silu(mixed).astype(jnp.bfloat16)
            gate = projected[:, :features].astype(jnp.float32)
            arrive(layer_index)
            values_all = jnp.where(
                in_history, hist_ref[layer_index, :, features:], jnp.zeros((), jnp.bfloat16)
            )
            heads = []
            for head in range(HEADS):
                low = head * head_dim
                query = projected[:, features + low:features + low + head_dim]
                keys = hist_ref[layer_index, :, low:low + head_dim]
                scores = lax.dot_general(
                    query, keys, (((1,), (1,)), ((), ())), preferred_element_type=jnp.float32
                )
                weight = silu(scores * factor).astype(jnp.bfloat16)
                heads.append(
                    jnp.dot(
                        weight,
                        values_all[:, low:low + head_dim],
                        preferred_element_type=jnp.float32,
                    )
                )
            attended = jnp.concatenate(heads, axis=1)
            branch = (layer_normed(attended) * gate).astype(jnp.bfloat16)
            if layer_index == 0:
                arrive(layer_count)
            residual = residual + jnp.dot(
                branch, w_out_ref[layer_index], preferred_element_type=jnp.float32
            )
        out_ref[...] = (residual - start).reshape(sources, slots, features).astype(out_ref.dtype)


def run_layers(buckets, history, length, w_in, w_out):
    sources, capacity, features = buckets.shape
    layer_count, history_span, width = history.shape
    steps = capacity // SLOT_BLOCK
    busy = jnp.any(
        buckets.reshape(sources, steps, SLOT_BLOCK * features) != 0, axis=(0, 2)
    ).astype(jnp.int32)
    grid_spec = pltpu.PrefetchScalarGridSpec(
        num_scalar_prefetch=2,
        grid=(steps,),
        in_specs=[
            pl.BlockSpec((sources, SLOT_BLOCK, features), lambda i, n, b: (0, i, 0)),
            pl.BlockSpec(w_in.shape, lambda i, n, b: (0, 0, 0)),
            pl.BlockSpec(memory_space=pltpu.MemorySpace.HBM),
            pl.BlockSpec(memory_space=pltpu.MemorySpace.HBM),
        ],
        out_specs=pl.BlockSpec((sources, SLOT_BLOCK, features), lambda i, n, b: (0, i, 0)),
        scratch_shapes=[
            pltpu.VMEM(history.shape, history.dtype),
            pltpu.VMEM(w_out.shape, w_out.dtype),
            pltpu.SemaphoreType.DMA((layer_count + 1,)),
        ],
    )
    row_count = sources * capacity
    flops = 2 * row_count * layer_count * (
        features * 2 * features + 2 * history_span * features + features * features
    )
    return pl.pallas_call(
        layers_kernel,
        grid_spec=grid_spec,
        out_shape=jax.ShapeDtypeStruct(buckets.shape, jnp.bfloat16),
        compiler_params=pltpu.CompilerParams(
            dimension_semantics=("arbitrary",), vmem_limit_bytes=48 * 1024 * 1024
        ),
        cost_estimate=pl.CostEstimate(
            flops=flops,
            transcendentals=row_count * layer_count * (HEADS * history_span + 2 * features),
            bytes_accessed=2 * (history.size + w_in.size + w_out.size + 2 * buckets.size),
        ),
    )(length, busy, buckets, w_in, history, w_out)


def pack_kernel(route_ref, emb_ref, packed_ref, position_ref, *, group_size, user_count):
    cand_rows = emb_ref.shape[0]
    capacity = packed_ref.shape[0] // user_count
    owner = route_ref[...] // group_size
    member = (lax.broadcasted_iota(jnp.int32, (user_count, cand_rows), 0) == owner).astype(
        jnp.float32
    )
    earlier = (
        lax.broadcasted_iota(jnp.int32, (cand_rows, cand_rows), 0)
        < lax.broadcasted_iota(jnp.int32, (cand_rows, cand_rows), 1)
    ).astype(jnp.bfloat16)
    before = jnp.dot(member.astype(jnp.bfloat16), earlier, preferred_element_type=jnp.float32)
    ranking = jnp.sum(member * before, axis=0, keepdims=True).astype(jnp.int32)
    position = owner * capacity + ranking
    position_ref[...] = position
    placing = (
        lax.broadcasted_iota(jnp.int32, (packed_ref.shape[0], cand_rows), 0) == position
    ).astype(jnp.bfloat16)
    packed_ref[...] = jnp.dot(
        placing, emb_ref[...], preferred_element_type=jnp.float32
    ).astype(packed_ref.dtype)


def pack_rows(cand_emb, cand_route, user_count, group_size):
    cand_rows, features = cand_emb.shape
    slots = 2 * cand_rows
    return pl.pallas_call(
        functools.partial(pack_kernel, group_size=group_size, user_count=user_count),
        out_shape=(
            jax.ShapeDtypeStruct((slots, features), jnp.bfloat16),
            jax.ShapeDtypeStruct((1, cand_rows), jnp.int32),
        ),
        in_specs=[pl.BlockSpec(memory_space=pltpu.VMEM)] * 2,
        out_specs=(pl.BlockSpec(memory_space=pltpu.VMEM),) * 2,
        cost_estimate=pl.CostEstimate(
            flops=2 * slots * cand_rows * features + 2 * user_count * cand_rows * cand_rows,
            transcendentals=0,
            bytes_accessed=2 * (cand_emb.size + slots * features),
        ),
    )(cand_route.reshape(1, cand_rows), cand_emb)


def local(cand_emb, cand_route, hist_kv, hist_len, w_in, w_out):
    cand_rows, features = cand_emb.shape
    user_count = lax.axis_size("user")
    group_size = lax.axis_size("cand")
    packed, position = pack_rows(cand_emb, cand_route, user_count, group_size)
    slots = packed.shape[0]
    capacity = slots // user_count
    placing = (lax.broadcasted_iota(jnp.int32, (slots, cand_rows), 0) == position).astype(
        jnp.bfloat16
    )
    outgoing = packed.reshape(user_count, capacity, features)
    items = lax.all_to_all(outgoing, "user", split_axis=0, concat_axis=0, tiled=True)
    history = hist_kv.reshape(hist_kv.shape[0], hist_kv.shape[2], hist_kv.shape[3])
    delta = run_layers(items, history, hist_len, w_in, w_out)
    returned = lax.all_to_all(delta, "user", split_axis=0, concat_axis=0, tiled=True)
    gathered = lax.dot_general(
        placing,
        returned.reshape(-1, features),
        (((0,), (0,)), ((), ())),
        preferred_element_type=jnp.float32,
    )
    return cand_emb.astype(jnp.float32) + gathered


def solution(mesh):
    placed = (
        P(("user", "cand"), None),
        P(("user", "cand")),
        P(None, "user", None, None),
        P("user"),
        P(),
        P(),
    )
    return jax.shard_map(
        local, mesh=mesh, in_specs=placed, out_specs=P(("user", "cand"), None), check_vma=False
    )
```

```python
import functools

import jax
import jax.numpy as jnp
from jax import lax
from jax.experimental import pallas as pl
from jax.experimental.pallas import tpu as pltpu
from jax.sharding import PartitionSpec as P

HEADS = 4
SLOT_BLOCK = 16

epsilon = 1e-05


def silu(v):
    return v * jax.nn.sigmoid(v)


def layer_normed(values):
    center = values - jnp.mean(values, axis=-1, keepdims=True)
    spread = jnp.mean(center * center, axis=-1, keepdims=True)
    return center * lax.rsqrt(spread + epsilon)


def layers_kernel(
    length_ref, busy_ref, rows_ref, w_in_ref, hist_hbm, w_out_hbm, out_ref, hist_ref, w_out_ref,
    copy_sems,
):
    sources, slots, features = rows_ref.shape
    block_rows = sources * slots
    layer_count = w_in_ref.shape[0]
    history_span = hist_ref.shape[1]
    head_dim = features // HEADS
    factor = head_dim ** (-0.5)
    step = pl.program_id(0)
    copies = [
        pltpu.make_async_copy(hist_hbm.at[layer], hist_ref.at[layer], copy_sems.at[layer])
        for layer in range(layer_count)
    ]
    copies.append(pltpu.make_async_copy(w_out_hbm, w_out_ref, copy_sems.at[layer_count]))

    @pl.when(step == 0)
    def _():
        for copy in copies:
            copy.start()

    def arrive(index):
        @pl.when(step == 0)
        def _():
            copies[index].wait()

    @pl.when(busy_ref[step] == 0)
    def _():
        out_ref[...] = jnp.zeros(out_ref.shape, out_ref.dtype)
        for index in range(len(copies)):
            arrive(index)

    @pl.when(busy_ref[step] != 0)
    def _():
        length = length_ref[0]
        in_history = lax.broadcasted_iota(jnp.int32, (history_span, 1), 0) < length
        start = rows_ref[...].astype(jnp.float32).reshape(block_rows, features)
        residual = start
        for layer_index in range(layer_count):
            normed = layer_normed(residual).astype(jnp.bfloat16)
            mixed = jnp.dot(normed, w_in_ref[layer_index], preferred_element_type=jnp.float32)
            projected = silu(mixed).astype(jnp.bfloat16)
            gate = projected[:, :features].astype(jnp.float32)
            arrive(layer_index)
            values_all = jnp.where(
                in_history, hist_ref[layer_index, :, features:], jnp.zeros((), jnp.bfloat16)
            )
            heads = []
            for head in range(HEADS):
                low = head * head_dim
                query = projected[:, features + low:features + low + head_dim]
                keys = hist_ref[layer_index, :, low:low + head_dim]
                scores = lax.dot_general(
                    query, keys, (((1,), (1,)), ((), ())), preferred_element_type=jnp.float32
                )
                weight = silu(scores * factor).astype(jnp.bfloat16)
                heads.append(
                    jnp.dot(
                        weight,
                        values_all[:, low:low + head_dim],
                        preferred_element_type=jnp.float32,
                    )
                )
            attended = jnp.concatenate(heads, axis=1)
            branch = (layer_normed(attended) * gate).astype(jnp.bfloat16)
            if layer_index == 0:
                arrive(layer_count)
            residual = residual + jnp.dot(
                branch, w_out_ref[layer_index], preferred_element_type=jnp.float32
            )
        out_ref[...] = (residual - start).reshape(sources, slots, features).astype(out_ref.dtype)


def run_layers(buckets, history, length, w_in, w_out):
    sources, capacity, features = buckets.shape
    layer_count, history_span, width = history.shape
    steps = capacity // SLOT_BLOCK
    busy = jnp.any(
        buckets.reshape(sources, steps, SLOT_BLOCK * features) != 0, axis=(0, 2)
    ).astype(jnp.int32)
    grid_spec = pltpu.PrefetchScalarGridSpec(
        num_scalar_prefetch=2,
        grid=(steps,),
        in_specs=[
            pl.BlockSpec((sources, SLOT_BLOCK, features), lambda i, n, b: (0, i, 0)),
            pl.BlockSpec(w_in.shape, lambda i, n, b: (0, 0, 0)),
            pl.BlockSpec(memory_space=pltpu.MemorySpace.HBM),
            pl.BlockSpec(memory_space=pltpu.MemorySpace.HBM),
        ],
        out_specs=pl.BlockSpec((sources, SLOT_BLOCK, features), lambda i, n, b: (0, i, 0)),
        scratch_shapes=[
            pltpu.VMEM(history.shape, history.dtype),
            pltpu.VMEM(w_out.shape, w_out.dtype),
            pltpu.SemaphoreType.DMA((layer_count + 1,)),
        ],
    )
    row_count = sources * capacity
    flops = 2 * row_count * layer_count * (
        features * 2 * features + 2 * history_span * features + features * features
    )
    return pl.pallas_call(
        layers_kernel,
        grid_spec=grid_spec,
        out_shape=jax.ShapeDtypeStruct(buckets.shape, jnp.bfloat16),
        compiler_params=pltpu.CompilerParams(
            dimension_semantics=("arbitrary",), vmem_limit_bytes=48 * 1024 * 1024
        ),
        cost_estimate=pl.CostEstimate(
            flops=flops,
            transcendentals=row_count * layer_count * (HEADS * history_span + 2 * features),
            bytes_accessed=2 * (history.size + w_in.size + w_out.size + 2 * buckets.size),
        ),
    )(length, busy, buckets, w_in, history, w_out)


def rank_of(route, group_size, user_count, capacity):
    cand_rows = route.shape[1]
    owner = route // group_size
    member = (lax.broadcasted_iota(jnp.int32, (user_count, cand_rows), 0) == owner).astype(
        jnp.float32
    )
    earlier = (
        lax.broadcasted_iota(jnp.int32, (cand_rows, cand_rows), 0)
        < lax.broadcasted_iota(jnp.int32, (cand_rows, cand_rows), 1)
    ).astype(jnp.bfloat16)
    before = jnp.dot(member.astype(jnp.bfloat16), earlier, preferred_element_type=jnp.float32)
    ranking = jnp.sum(member * before, axis=0, keepdims=True).astype(jnp.int32)
    return owner * capacity + ranking


def position_kernel(route_ref, position_ref, *, group_size, user_count, capacity):
    position_ref[...] = rank_of(route_ref[...], group_size, user_count, capacity)


def pack_kernel(route_ref, emb_ref, packed_ref, *, group_size, user_count):
    cand_rows = emb_ref.shape[0]
    capacity = packed_ref.shape[0] // user_count
    position = rank_of(route_ref[...], group_size, user_count, capacity)
    placing = (
        lax.broadcasted_iota(jnp.int32, (packed_ref.shape[0], cand_rows), 0) == position
    ).astype(jnp.bfloat16)
    packed_ref[...] = jnp.dot(
        placing, emb_ref[...], preferred_element_type=jnp.float32
    ).astype(packed_ref.dtype)


def pack_rows(cand_emb, cand_route, user_count, group_size):
    cand_rows, features = cand_emb.shape
    slots = 2 * cand_rows
    route = cand_route.reshape(1, cand_rows)
    packed = pl.pallas_call(
        functools.partial(pack_kernel, group_size=group_size, user_count=user_count),
        out_shape=jax.ShapeDtypeStruct((slots, features), jnp.bfloat16),
        in_specs=[pl.BlockSpec(memory_space=pltpu.VMEM)] * 2,
        out_specs=pl.BlockSpec(memory_space=pltpu.VMEM),
        cost_estimate=pl.CostEstimate(
            flops=2 * slots * cand_rows * features + 2 * user_count * cand_rows * cand_rows,
            transcendentals=0,
            bytes_accessed=2 * (cand_emb.size + slots * features),
        ),
    )(route, cand_emb)
    position = pl.pallas_call(
        functools.partial(
            position_kernel,
            group_size=group_size,
            user_count=user_count,
            capacity=slots // user_count,
        ),
        out_shape=jax.ShapeDtypeStruct((1, cand_rows), jnp.int32),
        in_specs=[pl.BlockSpec(memory_space=pltpu.VMEM)],
        out_specs=pl.BlockSpec(memory_space=pltpu.VMEM),
        cost_estimate=pl.CostEstimate(
            flops=2 * user_count * cand_rows * cand_rows,
            transcendentals=0,
            bytes_accessed=8 * cand_rows,
        ),
    )(route)
    return packed, position


def local(cand_emb, cand_route, hist_kv, hist_len, w_in, w_out):
    cand_rows, features = cand_emb.shape
    user_count = lax.axis_size("user")
    group_size = lax.axis_size("cand")
    packed, position = pack_rows(cand_emb, cand_route, user_count, group_size)
    slots = packed.shape[0]
    capacity = slots // user_count
    placing = (lax.broadcasted_iota(jnp.int32, (slots, cand_rows), 0) == position).astype(
        jnp.bfloat16
    )
    outgoing = packed.reshape(user_count, capacity, features)
    items = lax.all_to_all(outgoing, "user", split_axis=0, concat_axis=0, tiled=True)
    history = hist_kv.reshape(hist_kv.shape[0], hist_kv.shape[2], hist_kv.shape[3])
    delta = run_layers(items, history, hist_len, w_in, w_out)
    returned = lax.all_to_all(delta, "user", split_axis=0, concat_axis=0, tiled=True)
    gathered = lax.dot_general(
        placing,
        returned.reshape(-1, features),
        (((0,), (0,)), ((), ())),
        preferred_element_type=jnp.float32,
    )
    return cand_emb.astype(jnp.float32) + gathered


def solution(mesh):
    placed = (
        P(("user", "cand"), None),
        P(("user", "cand")),
        P(None, "user", None, None),
        P("user"),
        P(),
        P(),
    )
    return jax.shard_map(
        local, mesh=mesh, in_specs=placed, out_specs=P(("user", "cand"), None), check_vma=False
    )
```

```python
import functools

import jax
import jax.numpy as jnp
from jax import lax
from jax.experimental import pallas as pl
from jax.experimental.pallas import tpu as pltpu
from jax.sharding import PartitionSpec as P

HEADS = 4
SLOT_BLOCK = 16

epsilon = 1e-05


def silu(v):
    return v * jax.nn.sigmoid(v)


def layer_normed(values):
    center = values - jnp.mean(values, axis=-1, keepdims=True)
    spread = jnp.mean(center * center, axis=-1, keepdims=True)
    return center * lax.rsqrt(spread + epsilon)


def layers_kernel(length_ref, busy_ref, rows_ref, w_in_ref, tables_hbm, out_ref, tables_ref, copy_sems):
    sources, slots, features = rows_ref.shape
    block_rows = sources * slots
    layer_count = w_in_ref.shape[0]
    history_span = tables_ref.shape[1] - features
    head_dim = features // HEADS
    factor = head_dim ** (-0.5)
    step = pl.program_id(0)
    copies = [
        pltpu.make_async_copy(tables_hbm.at[layer], tables_ref.at[layer], copy_sems.at[layer])
        for layer in range(layer_count)
    ]

    @pl.when(step == 0)
    def _():
        for copy in copies:
            copy.start()

    def arrive(index):
        @pl.when(step == 0)
        def _():
            copies[index].wait()

    @pl.when(busy_ref[step] == 0)
    def _():
        out_ref[...] = jnp.zeros(out_ref.shape, out_ref.dtype)
        for index in range(len(copies)):
            arrive(index)

    @pl.when(busy_ref[step] != 0)
    def _():
        start = rows_ref[...].astype(jnp.float32).reshape(block_rows, features)
        residual = start
        for layer_index in range(layer_count):
            normed = layer_normed(residual).astype(jnp.bfloat16)
            mixed = jnp.dot(normed, w_in_ref[layer_index], preferred_element_type=jnp.float32)
            projected = silu(mixed).astype(jnp.bfloat16)
            gate = projected[:, :features].astype(jnp.float32)
            arrive(layer_index)
            heads = []
            for head in range(HEADS):
                low = head * head_dim
                query = projected[:, features + low:features + low + head_dim]
                keys = tables_ref[layer_index, :history_span, low:low + head_dim]
                scores = lax.dot_general(
                    query, keys, (((1,), (1,)), ((), ())), preferred_element_type=jnp.float32
                )
                weight = silu(scores * factor).astype(jnp.bfloat16)
                heads.append(
                    jnp.dot(
                        weight,
                        tables_ref[
                            layer_index, :history_span, features + low:features + low + head_dim
                        ],
                        preferred_element_type=jnp.float32,
                    )
                )
            attended = jnp.concatenate(heads, axis=1)
            branch = (layer_normed(attended) * gate).astype(jnp.bfloat16)
            residual = residual + jnp.dot(
                branch,
                tables_ref[layer_index, history_span:, :features],
                preferred_element_type=jnp.float32,
            )
        out_ref[...] = (residual - start).reshape(sources, slots, features).astype(out_ref.dtype)


def run_layers(buckets, history, length, w_in, w_out):
    sources, capacity, features = buckets.shape
    layer_count, history_span, width = history.shape
    in_history = lax.broadcasted_iota(jnp.int32, (1, history_span, 1), 1) < length[0]
    tables = jnp.concatenate(
        [
            history[:, :, :features],
            jnp.where(in_history, history[:, :, features:], jnp.zeros((), history.dtype)),
        ],
        axis=2,
    )
    tables = jnp.concatenate(
        [tables, jnp.pad(w_out, ((0, 0), (0, 0), (0, width - features)))], axis=1
    )
    steps = capacity // SLOT_BLOCK
    busy = jnp.any(
        buckets.reshape(sources, steps, SLOT_BLOCK * features) != 0, axis=(0, 2)
    ).astype(jnp.int32)
    grid_spec = pltpu.PrefetchScalarGridSpec(
        num_scalar_prefetch=2,
        grid=(steps,),
        in_specs=[
            pl.BlockSpec((sources, SLOT_BLOCK, features), lambda i, n, b: (0, i, 0)),
            pl.BlockSpec(w_in.shape, lambda i, n, b: (0, 0, 0)),
            pl.BlockSpec(memory_space=pltpu.MemorySpace.HBM),
        ],
        out_specs=pl.BlockSpec((sources, SLOT_BLOCK, features), lambda i, n, b: (0, i, 0)),
        scratch_shapes=[
            pltpu.VMEM(tables.shape, tables.dtype),
            pltpu.SemaphoreType.DMA((layer_count,)),
        ],
    )
    row_count = sources * capacity
    flops = 2 * row_count * layer_count * (
        features * 2 * features + 2 * history_span * features + features * features
    )
    return pl.pallas_call(
        layers_kernel,
        grid_spec=grid_spec,
        out_shape=jax.ShapeDtypeStruct(buckets.shape, jnp.bfloat16),
        compiler_params=pltpu.CompilerParams(
            dimension_semantics=("arbitrary",), vmem_limit_bytes=48 * 1024 * 1024
        ),
        cost_estimate=pl.CostEstimate(
            flops=flops,
            transcendentals=row_count * layer_count * (HEADS * history_span + 2 * features),
            bytes_accessed=2 * (history.size + w_in.size + w_out.size + 2 * buckets.size),
        ),
    )(length, busy, buckets, w_in, tables)


def pack_kernel(route_ref, emb_ref, packed_ref, position_ref, *, group_size, user_count):
    cand_rows = emb_ref.shape[0]
    capacity = packed_ref.shape[0] // user_count
    owner = route_ref[...] // group_size
    member = (lax.broadcasted_iota(jnp.int32, (user_count, cand_rows), 0) == owner).astype(
        jnp.float32
    )
    earlier = (
        lax.broadcasted_iota(jnp.int32, (cand_rows, cand_rows), 0)
        < lax.broadcasted_iota(jnp.int32, (cand_rows, cand_rows), 1)
    ).astype(jnp.bfloat16)
    before = jnp.dot(member.astype(jnp.bfloat16), earlier, preferred_element_type=jnp.float32)
    ranking = jnp.sum(member * before, axis=0, keepdims=True).astype(jnp.int32)
    position = owner * capacity + ranking
    position_ref[...] = position
    placing = (
        lax.broadcasted_iota(jnp.int32, (packed_ref.shape[0], cand_rows), 0) == position
    ).astype(jnp.bfloat16)
    packed_ref[...] = jnp.dot(
        placing, emb_ref[...], preferred_element_type=jnp.float32
    ).astype(packed_ref.dtype)


def pack_rows(cand_emb, cand_route, user_count, group_size):
    cand_rows, features = cand_emb.shape
    slots = 2 * cand_rows
    return pl.pallas_call(
        functools.partial(pack_kernel, group_size=group_size, user_count=user_count),
        out_shape=(
            jax.ShapeDtypeStruct((slots, features), jnp.bfloat16),
            jax.ShapeDtypeStruct((1, cand_rows), jnp.int32),
        ),
        in_specs=[pl.BlockSpec(memory_space=pltpu.VMEM)] * 2,
        out_specs=(pl.BlockSpec(memory_space=pltpu.VMEM),) * 2,
        cost_estimate=pl.CostEstimate(
            flops=2 * slots * cand_rows * features + 2 * user_count * cand_rows * cand_rows,
            transcendentals=0,
            bytes_accessed=2 * (cand_emb.size + slots * features),
        ),
    )(cand_route.reshape(1, cand_rows), cand_emb)


def local(cand_emb, cand_route, hist_kv, hist_len, w_in, w_out):
    cand_rows, features = cand_emb.shape
    user_count = lax.axis_size("user")
    group_size = lax.axis_size("cand")
    packed, position = pack_rows(cand_emb, cand_route, user_count, group_size)
    slots = packed.shape[0]
    capacity = slots // user_count
    placing = (lax.broadcasted_iota(jnp.int32, (slots, cand_rows), 0) == position).astype(
        jnp.bfloat16
    )
    outgoing = packed.reshape(user_count, capacity, features)
    items = lax.all_to_all(outgoing, "user", split_axis=0, concat_axis=0, tiled=True)
    history = hist_kv.reshape(hist_kv.shape[0], hist_kv.shape[2], hist_kv.shape[3])
    delta = run_layers(items, history, hist_len, w_in, w_out)
    returned = lax.all_to_all(delta, "user", split_axis=0, concat_axis=0, tiled=True)
    gathered = lax.dot_general(
        placing,
        returned.reshape(-1, features),
        (((0,), (0,)), ((), ())),
        preferred_element_type=jnp.float32,
    )
    return cand_emb.astype(jnp.float32) + gathered


def solution(mesh):
    placed = (
        P(("user", "cand"), None),
        P(("user", "cand")),
        P(None, "user", None, None),
        P("user"),
        P(),
        P(),
    )
    return jax.shard_map(
        local, mesh=mesh, in_specs=placed, out_specs=P(("user", "cand"), None), check_vma=False
    )
```

```python
import functools

import jax
import jax.numpy as jnp
from jax import lax
from jax.experimental import pallas as pl
from jax.experimental.pallas import tpu as pltpu
from jax.sharding import PartitionSpec as P

HEADS = 4
SLOT_BLOCK = 16

epsilon = 1e-05


def silu(v):
    return v * jax.nn.sigmoid(v)


def layer_normed(values):
    center = values - jnp.mean(values, axis=-1, keepdims=True)
    spread = jnp.mean(center * center, axis=-1, keepdims=True)
    return center * lax.rsqrt(spread + epsilon)


def layers_kernel(rows_ref, w_in_ref, tables_hbm, out_ref, tables_ref, copy_sems):
    sources, slots, features = rows_ref.shape
    block_rows = sources * slots
    layer_count = w_in_ref.shape[0]
    history_span = tables_ref.shape[1] - features
    head_dim = features // HEADS
    factor = head_dim ** (-0.5)
    step = pl.program_id(0)
    copies = [
        pltpu.make_async_copy(tables_hbm.at[layer], tables_ref.at[layer], copy_sems.at[layer])
        for layer in range(layer_count)
    ]

    @pl.when(step == 0)
    def _():
        for copy in copies:
            copy.start()

    def arrive(index):
        @pl.when(step == 0)
        def _():
            copies[index].wait()

    busy = jnp.max(jnp.abs(rows_ref[...].astype(jnp.float32))) > 0

    @pl.when(jnp.logical_not(busy))
    def _():
        out_ref[...] = jnp.zeros(out_ref.shape, out_ref.dtype)
        for index in range(len(copies)):
            arrive(index)

    @pl.when(busy)
    def _():
        start = rows_ref[...].astype(jnp.float32).reshape(block_rows, features)
        residual = start
        for layer_index in range(layer_count):
            normed = layer_normed(residual).astype(jnp.bfloat16)
            mixed = jnp.dot(normed, w_in_ref[layer_index], preferred_element_type=jnp.float32)
            projected = silu(mixed).astype(jnp.bfloat16)
            gate = projected[:, :features].astype(jnp.float32)
            arrive(layer_index)
            heads = []
            for head in range(HEADS):
                low = head * head_dim
                query = projected[:, features + low:features + low + head_dim]
                keys = tables_ref[layer_index, :history_span, low:low + head_dim]
                scores = lax.dot_general(
                    query, keys, (((1,), (1,)), ((), ())), preferred_element_type=jnp.float32
                )
                weight = silu(scores * factor).astype(jnp.bfloat16)
                heads.append(
                    jnp.dot(
                        weight,
                        tables_ref[
                            layer_index, :history_span, features + low:features + low + head_dim
                        ],
                        preferred_element_type=jnp.float32,
                    )
                )
            attended = jnp.concatenate(heads, axis=1)
            branch = (layer_normed(attended) * gate).astype(jnp.bfloat16)
            residual = residual + jnp.dot(
                branch,
                tables_ref[layer_index, history_span:, :features],
                preferred_element_type=jnp.float32,
            )
        out_ref[...] = (residual - start).reshape(sources, slots, features).astype(out_ref.dtype)


def run_layers(buckets, history, length, w_in, w_out):
    sources, capacity, features = buckets.shape
    layer_count, history_span, width = history.shape
    in_history = lax.broadcasted_iota(jnp.int32, (1, history_span, 1), 1) < length[0]
    tables = jnp.concatenate(
        [
            history[:, :, :features],
            jnp.where(in_history, history[:, :, features:], jnp.zeros((), history.dtype)),
        ],
        axis=2,
    )
    tables = jnp.concatenate(
        [tables, jnp.pad(w_out, ((0, 0), (0, 0), (0, width - features)))], axis=1
    )
    steps = capacity // SLOT_BLOCK
    grid_spec = pltpu.PrefetchScalarGridSpec(
        num_scalar_prefetch=0,
        grid=(steps,),
        in_specs=[
            pl.BlockSpec((sources, SLOT_BLOCK, features), lambda i: (0, i, 0)),
            pl.BlockSpec(w_in.shape, lambda i: (0, 0, 0)),
            pl.BlockSpec(memory_space=pltpu.MemorySpace.HBM),
        ],
        out_specs=pl.BlockSpec((sources, SLOT_BLOCK, features), lambda i: (0, i, 0)),
        scratch_shapes=[
            pltpu.VMEM(tables.shape, tables.dtype),
            pltpu.SemaphoreType.DMA((layer_count,)),
        ],
    )
    row_count = sources * capacity
    flops = 2 * row_count * layer_count * (
        features * 2 * features + 2 * history_span * features + features * features
    )
    return pl.pallas_call(
        layers_kernel,
        grid_spec=grid_spec,
        out_shape=jax.ShapeDtypeStruct(buckets.shape, jnp.bfloat16),
        compiler_params=pltpu.CompilerParams(
            dimension_semantics=("arbitrary",), vmem_limit_bytes=48 * 1024 * 1024
        ),
        cost_estimate=pl.CostEstimate(
            flops=flops,
            transcendentals=row_count * layer_count * (HEADS * history_span + 2 * features),
            bytes_accessed=2 * (history.size + w_in.size + w_out.size + 2 * buckets.size),
        ),
    )(buckets, w_in, tables)


def pack_kernel(route_ref, emb_ref, packed_ref, position_ref, *, group_size, user_count):
    cand_rows = emb_ref.shape[0]
    capacity = packed_ref.shape[0] // user_count
    owner = route_ref[...] // group_size
    member = (lax.broadcasted_iota(jnp.int32, (user_count, cand_rows), 0) == owner).astype(
        jnp.float32
    )
    earlier = (
        lax.broadcasted_iota(jnp.int32, (cand_rows, cand_rows), 0)
        < lax.broadcasted_iota(jnp.int32, (cand_rows, cand_rows), 1)
    ).astype(jnp.bfloat16)
    before = jnp.dot(member.astype(jnp.bfloat16), earlier, preferred_element_type=jnp.float32)
    ranking = jnp.sum(member * before, axis=0, keepdims=True).astype(jnp.int32)
    position = owner * capacity + ranking
    position_ref[...] = position
    placing = (
        lax.broadcasted_iota(jnp.int32, (packed_ref.shape[0], cand_rows), 0) == position
    ).astype(jnp.bfloat16)
    packed_ref[...] = jnp.dot(
        placing, emb_ref[...], preferred_element_type=jnp.float32
    ).astype(packed_ref.dtype)


def pack_rows(cand_emb, cand_route, user_count, group_size):
    cand_rows, features = cand_emb.shape
    slots = 2 * cand_rows
    return pl.pallas_call(
        functools.partial(pack_kernel, group_size=group_size, user_count=user_count),
        out_shape=(
            jax.ShapeDtypeStruct((slots, features), jnp.bfloat16),
            jax.ShapeDtypeStruct((1, cand_rows), jnp.int32),
        ),
        in_specs=[pl.BlockSpec(memory_space=pltpu.VMEM)] * 2,
        out_specs=(pl.BlockSpec(memory_space=pltpu.VMEM),) * 2,
        cost_estimate=pl.CostEstimate(
            flops=2 * slots * cand_rows * features + 2 * user_count * cand_rows * cand_rows,
            transcendentals=0,
            bytes_accessed=2 * (cand_emb.size + slots * features),
        ),
    )(cand_route.reshape(1, cand_rows), cand_emb)


def local(cand_emb, cand_route, hist_kv, hist_len, w_in, w_out):
    cand_rows, features = cand_emb.shape
    user_count = lax.axis_size("user")
    group_size = lax.axis_size("cand")
    packed, position = pack_rows(cand_emb, cand_route, user_count, group_size)
    slots = packed.shape[0]
    capacity = slots // user_count
    placing = (lax.broadcasted_iota(jnp.int32, (slots, cand_rows), 0) == position).astype(
        jnp.bfloat16
    )
    outgoing = packed.reshape(user_count, capacity, features)
    items = lax.all_to_all(outgoing, "user", split_axis=0, concat_axis=0, tiled=True)
    history = hist_kv.reshape(hist_kv.shape[0], hist_kv.shape[2], hist_kv.shape[3])
    delta = run_layers(items, history, hist_len, w_in, w_out)
    returned = lax.all_to_all(delta, "user", split_axis=0, concat_axis=0, tiled=True)
    gathered = lax.dot_general(
        placing,
        returned.reshape(-1, features),
        (((0,), (0,)), ((), ())),
        preferred_element_type=jnp.float32,
    )
    return cand_emb.astype(jnp.float32) + gathered


def solution(mesh):
    placed = (
        P(("user", "cand"), None),
        P(("user", "cand")),
        P(None, "user", None, None),
        P("user"),
        P(),
        P(),
    )
    return jax.shard_map(
        local, mesh=mesh, in_specs=placed, out_specs=P(("user", "cand"), None), check_vma=False
    )
```

```python
import functools

import jax
import jax.numpy as jnp
from jax import lax
from jax.experimental import pallas as pl
from jax.experimental.pallas import tpu as pltpu
from jax.sharding import PartitionSpec as P

HEADS = 4
SLOT_BLOCK = 16

epsilon = 1e-05


def silu(v):
    return v * jax.nn.sigmoid(v)


def layer_normed(values):
    center = values - jnp.mean(values, axis=-1, keepdims=True)
    spread = jnp.mean(center * center, axis=-1, keepdims=True)
    return center * lax.rsqrt(spread + epsilon)


def layers_kernel(rows_ref, w_in_ref, tables_hbm, out_ref, tables_ref, copy_sems):
    sources, slots, features = rows_ref.shape
    block_rows = sources * slots
    layer_count = w_in_ref.shape[0]
    history_span = (tables_ref.shape[1] - features) // 2
    head_dim = features // HEADS
    factor = head_dim ** (-0.5)
    step = pl.program_id(0)
    copies = [
        pltpu.make_async_copy(tables_hbm.at[layer], tables_ref.at[layer], copy_sems.at[layer])
        for layer in range(layer_count)
    ]

    @pl.when(step == 0)
    def _():
        for copy in copies:
            copy.start()

    def arrive(index):
        @pl.when(step == 0)
        def _():
            copies[index].wait()

    busy = jnp.max(jnp.abs(rows_ref[...].astype(jnp.float32))) > 0

    @pl.when(jnp.logical_not(busy))
    def _():
        out_ref[...] = jnp.zeros(out_ref.shape, out_ref.dtype)
        for index in range(len(copies)):
            arrive(index)

    @pl.when(busy)
    def _():
        start = rows_ref[...].astype(jnp.float32).reshape(block_rows, features)
        residual = start
        for layer_index in range(layer_count):
            normed = layer_normed(residual).astype(jnp.bfloat16)
            mixed = jnp.dot(normed, w_in_ref[layer_index], preferred_element_type=jnp.float32)
            projected = silu(mixed).astype(jnp.bfloat16)
            gate = projected[:, :features].astype(jnp.float32)
            arrive(layer_index)
            heads = []
            for head in range(HEADS):
                low = head * head_dim
                query = projected[:, features + low:features + low + head_dim]
                keys = tables_ref[layer_index, :history_span, low:low + head_dim]
                values = tables_ref[
                    layer_index, history_span:2 * history_span, low:low + head_dim
                ]
                scores = lax.dot_general(
                    query, keys, (((1,), (1,)), ((), ())), preferred_element_type=jnp.float32
                )
                weight = silu(scores * factor).astype(jnp.bfloat16)
                heads.append(
                    jnp.dot(
                        weight,
                        values,
                        preferred_element_type=jnp.float32,
                    )
                )
            attended = jnp.concatenate(heads, axis=1)
            branch = (layer_normed(attended) * gate).astype(jnp.bfloat16)
            residual = residual + jnp.dot(
                branch,
                tables_ref[layer_index, 2 * history_span:, :],
                preferred_element_type=jnp.float32,
            )
        out_ref[...] = (residual - start).reshape(sources, slots, features).astype(out_ref.dtype)


def run_layers(buckets, history, length, w_in, w_out):
    sources, capacity, features = buckets.shape
    layer_count, history_span, width = history.shape
    in_history = lax.broadcasted_iota(jnp.int32, (1, history_span, 1), 1) < length[0]
    tables = jnp.concatenate(
        [
            history[:, :, :features],
            jnp.where(in_history, history[:, :, features:], jnp.zeros((), history.dtype)),
            w_out,
        ],
        axis=1,
    )
    steps = capacity // SLOT_BLOCK
    grid_spec = pltpu.PrefetchScalarGridSpec(
        num_scalar_prefetch=0,
        grid=(steps,),
        in_specs=[
            pl.BlockSpec((sources, SLOT_BLOCK, features), lambda i: (0, i, 0)),
            pl.BlockSpec(w_in.shape, lambda i: (0, 0, 0)),
            pl.BlockSpec(memory_space=pltpu.MemorySpace.HBM),
        ],
        out_specs=pl.BlockSpec((sources, SLOT_BLOCK, features), lambda i: (0, i, 0)),
        scratch_shapes=[
            pltpu.VMEM(tables.shape, tables.dtype),
            pltpu.SemaphoreType.DMA((layer_count,)),
        ],
    )
    row_count = sources * capacity
    flops = 2 * row_count * layer_count * (
        features * 2 * features + 2 * history_span * features + features * features
    )
    return pl.pallas_call(
        layers_kernel,
        grid_spec=grid_spec,
        out_shape=jax.ShapeDtypeStruct(buckets.shape, jnp.bfloat16),
        compiler_params=pltpu.CompilerParams(
            dimension_semantics=("arbitrary",), vmem_limit_bytes=48 * 1024 * 1024
        ),
        cost_estimate=pl.CostEstimate(
            flops=flops,
            transcendentals=row_count * layer_count * (HEADS * history_span + 2 * features),
            bytes_accessed=2 * (history.size + w_in.size + w_out.size + 2 * buckets.size),
        ),
    )(buckets, w_in, tables)


def pack_kernel(route_ref, emb_ref, packed_ref, position_ref, *, group_size, user_count):
    cand_rows = emb_ref.shape[0]
    capacity = packed_ref.shape[0] // user_count
    owner = route_ref[...] // group_size
    member = (lax.broadcasted_iota(jnp.int32, (user_count, cand_rows), 0) == owner).astype(
        jnp.float32
    )
    earlier = (
        lax.broadcasted_iota(jnp.int32, (cand_rows, cand_rows), 0)
        < lax.broadcasted_iota(jnp.int32, (cand_rows, cand_rows), 1)
    ).astype(jnp.bfloat16)
    before = jnp.dot(member.astype(jnp.bfloat16), earlier, preferred_element_type=jnp.float32)
    ranking = jnp.sum(member * before, axis=0, keepdims=True).astype(jnp.int32)
    position = owner * capacity + ranking
    position_ref[...] = position
    placing = (
        lax.broadcasted_iota(jnp.int32, (packed_ref.shape[0], cand_rows), 0) == position
    ).astype(jnp.bfloat16)
    packed_ref[...] = jnp.dot(
        placing, emb_ref[...], preferred_element_type=jnp.float32
    ).astype(packed_ref.dtype)


def pack_rows(cand_emb, cand_route, user_count, group_size):
    cand_rows, features = cand_emb.shape
    slots = 2 * cand_rows
    return pl.pallas_call(
        functools.partial(pack_kernel, group_size=group_size, user_count=user_count),
        out_shape=(
            jax.ShapeDtypeStruct((slots, features), jnp.bfloat16),
            jax.ShapeDtypeStruct((1, cand_rows), jnp.int32),
        ),
        in_specs=[pl.BlockSpec(memory_space=pltpu.VMEM)] * 2,
        out_specs=(pl.BlockSpec(memory_space=pltpu.VMEM),) * 2,
        cost_estimate=pl.CostEstimate(
            flops=2 * slots * cand_rows * features + 2 * user_count * cand_rows * cand_rows,
            transcendentals=0,
            bytes_accessed=2 * (cand_emb.size + slots * features),
        ),
    )(cand_route.reshape(1, cand_rows), cand_emb)


def local(cand_emb, cand_route, hist_kv, hist_len, w_in, w_out):
    cand_rows, features = cand_emb.shape
    user_count = lax.axis_size("user")
    group_size = lax.axis_size("cand")
    packed, position = pack_rows(cand_emb, cand_route, user_count, group_size)
    slots = packed.shape[0]
    capacity = slots // user_count
    placing = (lax.broadcasted_iota(jnp.int32, (slots, cand_rows), 0) == position).astype(
        jnp.bfloat16
    )
    outgoing = packed.reshape(user_count, capacity, features)
    items = lax.all_to_all(outgoing, "user", split_axis=0, concat_axis=0, tiled=True)
    history = hist_kv.reshape(hist_kv.shape[0], hist_kv.shape[2], hist_kv.shape[3])
    delta = run_layers(items, history, hist_len, w_in, w_out)
    returned = lax.all_to_all(delta, "user", split_axis=0, concat_axis=0, tiled=True)
    gathered = lax.dot_general(
        placing,
        returned.reshape(-1, features),
        (((0,), (0,)), ((), ())),
        preferred_element_type=jnp.float32,
    )
    return cand_emb.astype(jnp.float32) + gathered


def solution(mesh):
    placed = (
        P(("user", "cand"), None),
        P(("user", "cand")),
        P(None, "user", None, None),
        P("user"),
        P(),
        P(),
    )
    return jax.shard_map(
        local, mesh=mesh, in_specs=placed, out_specs=P(("user", "cand"), None), check_vma=False
    )
```

```python
import functools

import jax
import jax.numpy as jnp
from jax import lax
from jax.experimental import pallas as pl
from jax.experimental.pallas import tpu as pltpu
from jax.sharding import PartitionSpec as P

HEADS = 4
SLOT_BLOCK = 16

epsilon = 1e-05


def silu(v):
    return v * jax.nn.sigmoid(v)


def layer_normed(values):
    center = values - jnp.mean(values, axis=-1, keepdims=True)
    spread = jnp.mean(center * center, axis=-1, keepdims=True)
    return center * lax.rsqrt(spread + epsilon)


def layers_kernel(rows_ref, w_in_ref, tables_hbm, out_ref, tables_ref, copy_sems):
    sources, slots, features = rows_ref.shape
    block_rows = sources * slots
    layer_count = w_in_ref.shape[0]
    history_span = (tables_ref.shape[1] - features) // 2
    head_dim = features // HEADS
    factor = head_dim ** (-0.5)
    step = pl.program_id(0)
    copies = [
        pltpu.make_async_copy(tables_hbm.at[layer], tables_ref.at[layer], copy_sems.at[layer])
        for layer in range(layer_count)
    ]

    @pl.when(step == 0)
    def _():
        for copy in copies:
            copy.start()

    def arrive(index):
        @pl.when(step == 0)
        def _():
            copies[index].wait()

    busy = jnp.max(jnp.abs(rows_ref[...].astype(jnp.float32))) > 0

    @pl.when(jnp.logical_not(busy))
    def _():
        out_ref[...] = jnp.zeros(out_ref.shape, out_ref.dtype)
        for index in range(len(copies)):
            arrive(index)

    @pl.when(busy)
    def _():
        start = rows_ref[...].astype(jnp.float32).reshape(block_rows, features)
        residual = start
        for layer_index in range(layer_count):
            normed = layer_normed(residual).astype(jnp.bfloat16)
            mixed = jnp.dot(normed, w_in_ref[layer_index], preferred_element_type=jnp.float32)
            projected = silu(mixed).astype(jnp.bfloat16)
            gate = projected[:, :features].astype(jnp.float32)
            arrive(layer_index)
            heads = []
            for head in range(HEADS):
                low = head * head_dim
                query = projected[:, features + low:features + low + head_dim]
                keys = tables_ref[layer_index, :history_span, low:low + head_dim]
                values = tables_ref[
                    layer_index, history_span:2 * history_span, low:low + head_dim
                ]
                scores = lax.dot_general(
                    query, keys, (((1,), (1,)), ((), ())), preferred_element_type=jnp.float32
                )
                weight = silu(scores * factor).astype(jnp.bfloat16)
                heads.append(
                    jnp.dot(
                        weight,
                        values,
                        preferred_element_type=jnp.float32,
                    )
                )
            attended = jnp.concatenate(heads, axis=1)
            branch = (layer_normed(attended) * gate).astype(jnp.bfloat16)
            residual = residual + jnp.dot(
                branch,
                tables_ref[layer_index, 2 * history_span:, :],
                preferred_element_type=jnp.float32,
            )
        out_ref[...] = (residual - start).reshape(sources, slots, features).astype(out_ref.dtype)


def run_layers(buckets, history, length, w_in, w_out):
    sources, capacity, features = buckets.shape
    layer_count, history_span, width = history.shape
    in_history = lax.broadcasted_iota(jnp.int32, (1, history_span, 1), 1) < length[0]
    tables = jnp.concatenate(
        [
            history[:, :, :features],
            jnp.where(in_history, history[:, :, features:], jnp.zeros((), history.dtype)),
            w_out,
        ],
        axis=1,
    )
    steps = capacity // SLOT_BLOCK
    grid_spec = pltpu.PrefetchScalarGridSpec(
        num_scalar_prefetch=0,
        grid=(steps,),
        in_specs=[
            pl.BlockSpec((sources, SLOT_BLOCK, features), lambda i: (0, i, 0)),
            pl.BlockSpec(w_in.shape, lambda i: (0, 0, 0)),
            pl.BlockSpec(memory_space=pltpu.MemorySpace.HBM),
        ],
        out_specs=pl.BlockSpec((sources, SLOT_BLOCK, features), lambda i: (0, i, 0)),
        scratch_shapes=[
            pltpu.VMEM(tables.shape, tables.dtype),
            pltpu.SemaphoreType.DMA((layer_count,)),
        ],
    )
    row_count = sources * capacity
    flops = 2 * row_count * layer_count * (
        features * 2 * features + 2 * history_span * features + features * features
    )
    return pl.pallas_call(
        layers_kernel,
        grid_spec=grid_spec,
        out_shape=jax.ShapeDtypeStruct(buckets.shape, jnp.bfloat16),
        compiler_params=pltpu.CompilerParams(
            dimension_semantics=("arbitrary",), vmem_limit_bytes=48 * 1024 * 1024
        ),
        cost_estimate=pl.CostEstimate(
            flops=flops,
            transcendentals=row_count * layer_count * (HEADS * history_span + 2 * features),
            bytes_accessed=2 * (history.size + w_in.size + w_out.size + 2 * buckets.size),
        ),
    )(buckets, w_in, tables)


def pack_kernel(route_ref, emb_ref, packed_ref, position_ref, *, group_size, user_count):
    cand_rows = emb_ref.shape[0]
    block_slots = packed_ref.shape[0]
    capacity = 2 * cand_rows // user_count
    owner = route_ref[...] // group_size
    member = (lax.broadcasted_iota(jnp.int32, (user_count, cand_rows), 0) == owner).astype(
        jnp.float32
    )
    earlier = (
        lax.broadcasted_iota(jnp.int32, (cand_rows, cand_rows), 0)
        < lax.broadcasted_iota(jnp.int32, (cand_rows, cand_rows), 1)
    ).astype(jnp.bfloat16)
    before = jnp.dot(member.astype(jnp.bfloat16), earlier, preferred_element_type=jnp.float32)
    ranking = jnp.sum(member * before, axis=0, keepdims=True).astype(jnp.int32)
    position = owner * capacity + ranking
    position_ref[...] = position
    first = pl.program_id(0) * block_slots
    placing = (
        lax.broadcasted_iota(jnp.int32, (block_slots, cand_rows), 0) + first == position
    ).astype(jnp.bfloat16)
    packed_ref[...] = jnp.dot(
        placing, emb_ref[...], preferred_element_type=jnp.float32
    ).astype(packed_ref.dtype)


def pack_rows(cand_emb, cand_route, user_count, group_size):
    cand_rows, features = cand_emb.shape
    slots = 2 * cand_rows
    block_slots = slots // 4
    return pl.pallas_call(
        functools.partial(pack_kernel, group_size=group_size, user_count=user_count),
        grid=(slots // block_slots,),
        out_shape=(
            jax.ShapeDtypeStruct((slots, features), jnp.bfloat16),
            jax.ShapeDtypeStruct((1, cand_rows), jnp.int32),
        ),
        in_specs=[
            pl.BlockSpec((1, cand_rows), lambda i: (0, 0)),
            pl.BlockSpec((cand_rows, features), lambda i: (0, 0)),
        ],
        out_specs=(
            pl.BlockSpec((block_slots, features), lambda i: (i, 0)),
            pl.BlockSpec((1, cand_rows), lambda i: (0, 0)),
        ),
        compiler_params=pltpu.CompilerParams(dimension_semantics=("arbitrary",)),
        cost_estimate=pl.CostEstimate(
            flops=2 * slots * cand_rows * features + 8 * user_count * cand_rows * cand_rows,
            transcendentals=0,
            bytes_accessed=2 * (cand_emb.size + slots * features),
        ),
    )(cand_route.reshape(1, cand_rows), cand_emb)


def local(cand_emb, cand_route, hist_kv, hist_len, w_in, w_out):
    cand_rows, features = cand_emb.shape
    user_count = lax.axis_size("user")
    group_size = lax.axis_size("cand")
    packed, position = pack_rows(cand_emb, cand_route, user_count, group_size)
    slots = packed.shape[0]
    capacity = slots // user_count
    placing = (lax.broadcasted_iota(jnp.int32, (slots, cand_rows), 0) == position).astype(
        jnp.bfloat16
    )
    outgoing = packed.reshape(user_count, capacity, features)
    items = lax.all_to_all(outgoing, "user", split_axis=0, concat_axis=0, tiled=True)
    history = hist_kv.reshape(hist_kv.shape[0], hist_kv.shape[2], hist_kv.shape[3])
    delta = run_layers(items, history, hist_len, w_in, w_out)
    returned = lax.all_to_all(delta, "user", split_axis=0, concat_axis=0, tiled=True)
    gathered = lax.dot_general(
        placing,
        returned.reshape(-1, features),
        (((0,), (0,)), ((), ())),
        preferred_element_type=jnp.float32,
    )
    return cand_emb.astype(jnp.float32) + gathered


def solution(mesh):
    placed = (
        P(("user", "cand"), None),
        P(("user", "cand")),
        P(None, "user", None, None),
        P("user"),
        P(),
        P(),
    )
    return jax.shard_map(
        local, mesh=mesh, in_specs=placed, out_specs=P(("user", "cand"), None), check_vma=False
    )
```

```python
import functools

import jax
import jax.numpy as jnp
from jax import lax
from jax.experimental import pallas as pl
from jax.experimental.pallas import tpu as pltpu
from jax.sharding import PartitionSpec as P

HEADS = 4
SLOT_BLOCK = 16

epsilon = 1e-05


def silu(v):
    return v * jax.nn.sigmoid(v)


def layer_normed(values):
    center = values - jnp.mean(values, axis=-1, keepdims=True)
    spread = jnp.mean(center * center, axis=-1, keepdims=True)
    return center * lax.rsqrt(spread + epsilon)


def layers_kernel(
    rows_ref, w_in_ref, hist_hbm, tables_hbm, out_ref, keys_ref, tables_ref, copy_sems
):
    sources, slots, features = rows_ref.shape
    block_rows = sources * slots
    layer_count = w_in_ref.shape[0]
    history_span = keys_ref.shape[1]
    head_dim = features // HEADS
    factor = head_dim ** (-0.5)
    step = pl.program_id(0)
    copies = [
        (
            pltpu.make_async_copy(
                hist_hbm.at[layer, :, :features], keys_ref.at[layer], copy_sems.at[0, layer]
            ),
            pltpu.make_async_copy(
                tables_hbm.at[layer], tables_ref.at[layer], copy_sems.at[1, layer]
            ),
        )
        for layer in range(layer_count)
    ]

    @pl.when(step == 0)
    def _():
        for pair in copies:
            for copy in pair:
                copy.start()

    def arrive(index):
        @pl.when(step == 0)
        def _():
            for copy in copies[index]:
                copy.wait()

    busy = jnp.max(jnp.abs(rows_ref[...].astype(jnp.float32))) > 0

    @pl.when(jnp.logical_not(busy))
    def _():
        out_ref[...] = jnp.zeros(out_ref.shape, out_ref.dtype)
        for index in range(len(copies)):
            arrive(index)

    @pl.when(busy)
    def _():
        start = rows_ref[...].astype(jnp.float32).reshape(block_rows, features)
        residual = start
        for layer_index in range(layer_count):
            normed = layer_normed(residual).astype(jnp.bfloat16)
            mixed = jnp.dot(normed, w_in_ref[layer_index], preferred_element_type=jnp.float32)
            projected = silu(mixed).astype(jnp.bfloat16)
            gate = projected[:, :features].astype(jnp.float32)
            arrive(layer_index)
            heads = []
            for head in range(HEADS):
                low = head * head_dim
                query = projected[:, features + low:features + low + head_dim]
                keys = keys_ref[layer_index, :, low:low + head_dim]
                values = tables_ref[layer_index, :history_span, low:low + head_dim]
                scores = lax.dot_general(
                    query, keys, (((1,), (1,)), ((), ())), preferred_element_type=jnp.float32
                )
                weight = silu(scores * factor).astype(jnp.bfloat16)
                heads.append(
                    jnp.dot(
                        weight,
                        values,
                        preferred_element_type=jnp.float32,
                    )
                )
            attended = jnp.concatenate(heads, axis=1)
            branch = (layer_normed(attended) * gate).astype(jnp.bfloat16)
            residual = residual + jnp.dot(
                branch,
                tables_ref[layer_index, history_span:, :],
                preferred_element_type=jnp.float32,
            )
        out_ref[...] = (residual - start).reshape(sources, slots, features).astype(out_ref.dtype)


def run_layers(buckets, history, length, w_in, w_out):
    sources, capacity, features = buckets.shape
    layer_count, history_span, width = history.shape
    in_history = lax.broadcasted_iota(jnp.int32, (1, history_span, 1), 1) < length[0]
    tables = jnp.concatenate(
        [
            jnp.where(in_history, history[:, :, features:], jnp.zeros((), history.dtype)),
            w_out,
        ],
        axis=1,
    )
    steps = capacity // SLOT_BLOCK
    grid_spec = pltpu.PrefetchScalarGridSpec(
        num_scalar_prefetch=0,
        grid=(steps,),
        in_specs=[
            pl.BlockSpec((sources, SLOT_BLOCK, features), lambda i: (0, i, 0)),
            pl.BlockSpec(w_in.shape, lambda i: (0, 0, 0)),
            pl.BlockSpec(memory_space=pltpu.MemorySpace.HBM),
            pl.BlockSpec(memory_space=pltpu.MemorySpace.HBM),
        ],
        out_specs=pl.BlockSpec((sources, SLOT_BLOCK, features), lambda i: (0, i, 0)),
        scratch_shapes=[
            pltpu.VMEM((layer_count, history_span, features), history.dtype),
            pltpu.VMEM(tables.shape, tables.dtype),
            pltpu.SemaphoreType.DMA((2, layer_count)),
        ],
    )
    row_count = sources * capacity
    flops = 2 * row_count * layer_count * (
        features * 2 * features + 2 * history_span * features + features * features
    )
    return pl.pallas_call(
        layers_kernel,
        grid_spec=grid_spec,
        out_shape=jax.ShapeDtypeStruct(buckets.shape, jnp.bfloat16),
        compiler_params=pltpu.CompilerParams(
            dimension_semantics=("arbitrary",), vmem_limit_bytes=48 * 1024 * 1024
        ),
        cost_estimate=pl.CostEstimate(
            flops=flops,
            transcendentals=row_count * layer_count * (HEADS * history_span + 2 * features),
            bytes_accessed=2 * (history.size + w_in.size + w_out.size + 2 * buckets.size),
        ),
    )(buckets, w_in, history, tables)


def pack_kernel(route_ref, emb_ref, packed_ref, position_ref, *, group_size, user_count):
    cand_rows = emb_ref.shape[0]
    capacity = packed_ref.shape[0] // user_count
    owner = route_ref[...] // group_size
    member = (lax.broadcasted_iota(jnp.int32, (user_count, cand_rows), 0) == owner).astype(
        jnp.float32
    )
    earlier = (
        lax.broadcasted_iota(jnp.int32, (cand_rows, cand_rows), 0)
        < lax.broadcasted_iota(jnp.int32, (cand_rows, cand_rows), 1)
    ).astype(jnp.bfloat16)
    before = jnp.dot(member.astype(jnp.bfloat16), earlier, preferred_element_type=jnp.float32)
    ranking = jnp.sum(member * before, axis=0, keepdims=True).astype(jnp.int32)
    position = owner * capacity + ranking
    position_ref[...] = position
    placing = (
        lax.broadcasted_iota(jnp.int32, (packed_ref.shape[0], cand_rows), 0) == position
    ).astype(jnp.bfloat16)
    packed_ref[...] = jnp.dot(
        placing, emb_ref[...], preferred_element_type=jnp.float32
    ).astype(packed_ref.dtype)


def pack_rows(cand_emb, cand_route, user_count, group_size):
    cand_rows, features = cand_emb.shape
    slots = 2 * cand_rows
    return pl.pallas_call(
        functools.partial(pack_kernel, group_size=group_size, user_count=user_count),
        out_shape=(
            jax.ShapeDtypeStruct((slots, features), jnp.bfloat16),
            jax.ShapeDtypeStruct((1, cand_rows), jnp.int32),
        ),
        in_specs=[pl.BlockSpec(memory_space=pltpu.VMEM)] * 2,
        out_specs=(pl.BlockSpec(memory_space=pltpu.VMEM),) * 2,
        cost_estimate=pl.CostEstimate(
            flops=2 * slots * cand_rows * features + 2 * user_count * cand_rows * cand_rows,
            transcendentals=0,
            bytes_accessed=2 * (cand_emb.size + slots * features),
        ),
    )(cand_route.reshape(1, cand_rows), cand_emb)


def local(cand_emb, cand_route, hist_kv, hist_len, w_in, w_out):
    cand_rows, features = cand_emb.shape
    user_count = lax.axis_size("user")
    group_size = lax.axis_size("cand")
    packed, position = pack_rows(cand_emb, cand_route, user_count, group_size)
    slots = packed.shape[0]
    capacity = slots // user_count
    placing = (lax.broadcasted_iota(jnp.int32, (slots, cand_rows), 0) == position).astype(
        jnp.bfloat16
    )
    outgoing = packed.reshape(user_count, capacity, features)
    items = lax.all_to_all(outgoing, "user", split_axis=0, concat_axis=0, tiled=True)
    history = hist_kv.reshape(hist_kv.shape[0], hist_kv.shape[2], hist_kv.shape[3])
    delta = run_layers(items, history, hist_len, w_in, w_out)
    returned = lax.all_to_all(delta, "user", split_axis=0, concat_axis=0, tiled=True)
    gathered = lax.dot_general(
        placing,
        returned.reshape(-1, features),
        (((0,), (0,)), ((), ())),
        preferred_element_type=jnp.float32,
    )
    return cand_emb.astype(jnp.float32) + gathered


def solution(mesh):
    placed = (
        P(("user", "cand"), None),
        P(("user", "cand")),
        P(None, "user", None, None),
        P("user"),
        P(),
        P(),
    )
    return jax.shard_map(
        local, mesh=mesh, in_specs=placed, out_specs=P(("user", "cand"), None), check_vma=False
    )
```

```python
import functools

import jax
import jax.numpy as jnp
from jax import lax
from jax.experimental import pallas as pl
from jax.experimental.pallas import tpu as pltpu
from jax.sharding import PartitionSpec as P

HEADS = 4
SLOT_BLOCK = 16

epsilon = 1e-05


def silu(v):
    return v * jax.nn.sigmoid(v)


def layer_normed(values):
    center = values - jnp.mean(values, axis=-1, keepdims=True)
    spread = jnp.mean(center * center, axis=-1, keepdims=True)
    return center * lax.rsqrt(spread + epsilon)


def layers_kernel(rows_ref, w_in_ref, tables_hbm, out_ref, tables_ref, copy_sems):
    sources, slots, features = rows_ref.shape
    block_rows = sources * slots
    layer_count = w_in_ref.shape[0]
    history_span = (tables_ref.shape[1] - features) // 2
    head_dim = features // HEADS
    factor = head_dim ** (-0.5)
    step = pl.program_id(0)
    copies = [
        pltpu.make_async_copy(tables_hbm.at[layer], tables_ref.at[layer], copy_sems.at[layer])
        for layer in range(layer_count)
    ]

    @pl.when(step == 0)
    def _():
        for copy in copies:
            copy.start()

    def arrive(index):
        @pl.when(step == 0)
        def _():
            copies[index].wait()

    busy = jnp.max(jnp.abs(rows_ref[...].astype(jnp.float32))) > 0

    @pl.when(jnp.logical_not(busy))
    def _():
        out_ref[...] = jnp.zeros(out_ref.shape, out_ref.dtype)
        for index in range(len(copies)):
            arrive(index)

    @pl.when(busy)
    def _():
        start = rows_ref[...].astype(jnp.float32).reshape(block_rows, features)
        residual = start
        for layer_index in range(layer_count):
            normed = layer_normed(residual).astype(jnp.bfloat16)
            mixed = jnp.dot(normed, w_in_ref[layer_index], preferred_element_type=jnp.float32)
            projected = silu(mixed).astype(jnp.bfloat16)
            gate = projected[:, :features].astype(jnp.float32)
            arrive(layer_index)
            heads = []
            for head in range(HEADS):
                low = head * head_dim
                query = projected[:, features + low:features + low + head_dim]
                keys = tables_ref[layer_index, :history_span, low:low + head_dim]
                values = tables_ref[
                    layer_index, history_span:2 * history_span, low:low + head_dim
                ]
                scores = lax.dot_general(
                    query, keys, (((1,), (1,)), ((), ())), preferred_element_type=jnp.float32
                )
                weight = silu(scores * factor).astype(jnp.bfloat16)
                heads.append(
                    jnp.dot(
                        weight,
                        values,
                        preferred_element_type=jnp.float32,
                    )
                )
            attended = jnp.concatenate(heads, axis=1)
            branch = (layer_normed(attended) * gate).astype(jnp.bfloat16)
            residual = residual + jnp.dot(
                branch,
                tables_ref[layer_index, 2 * history_span:, :],
                preferred_element_type=jnp.float32,
            )
        out_ref[...] = (residual - start).reshape(sources, slots, features).astype(out_ref.dtype)


def run_layers(buckets, history, length, w_in, w_out):
    sources, capacity, features = buckets.shape
    layer_count, history_span, width = history.shape
    in_history = lax.broadcasted_iota(jnp.int32, (1, history_span, 1), 1) < length[0]
    tables = jnp.concatenate(
        [
            history[:, :, :features],
            jnp.where(in_history, history[:, :, features:], jnp.zeros((), history.dtype)),
            w_out,
        ],
        axis=1,
    )
    steps = capacity // SLOT_BLOCK
    grid_spec = pltpu.PrefetchScalarGridSpec(
        num_scalar_prefetch=0,
        grid=(steps,),
        in_specs=[
            pl.BlockSpec((sources, SLOT_BLOCK, features), lambda i: (0, i, 0)),
            pl.BlockSpec(w_in.shape, lambda i: (0, 0, 0)),
            pl.BlockSpec(memory_space=pltpu.MemorySpace.HBM),
        ],
        out_specs=pl.BlockSpec((sources, SLOT_BLOCK, features), lambda i: (0, i, 0)),
        scratch_shapes=[
            pltpu.VMEM(tables.shape, tables.dtype),
            pltpu.SemaphoreType.DMA((layer_count,)),
        ],
    )
    row_count = sources * capacity
    flops = 2 * row_count * layer_count * (
        features * 2 * features + 2 * history_span * features + features * features
    )
    return pl.pallas_call(
        layers_kernel,
        grid_spec=grid_spec,
        out_shape=jax.ShapeDtypeStruct(buckets.shape, jnp.bfloat16),
        compiler_params=pltpu.CompilerParams(
            dimension_semantics=("arbitrary",), vmem_limit_bytes=48 * 1024 * 1024
        ),
        cost_estimate=pl.CostEstimate(
            flops=flops,
            transcendentals=row_count * layer_count * (HEADS * history_span + 2 * features),
            bytes_accessed=2 * (history.size + w_in.size + w_out.size + 2 * buckets.size),
        ),
    )(buckets, w_in, tables)


def pack_kernel(
    route_ref, emb_ref, packed_ref, position_ref, placed_ref, *, group_size, user_count
):
    cand_rows = emb_ref.shape[0]
    block_slots = packed_ref.shape[0]
    capacity = 2 * cand_rows // user_count

    @pl.when(pl.program_id(0) == 0)
    def _():
        owner = route_ref[...] // group_size
        member = (
            lax.broadcasted_iota(jnp.int32, (user_count, cand_rows), 0) == owner
        ).astype(jnp.float32)
        earlier = (
            lax.broadcasted_iota(jnp.int32, (cand_rows, cand_rows), 0)
            < lax.broadcasted_iota(jnp.int32, (cand_rows, cand_rows), 1)
        ).astype(jnp.bfloat16)
        before = jnp.dot(
            member.astype(jnp.bfloat16), earlier, preferred_element_type=jnp.float32
        )
        ranking = jnp.sum(member * before, axis=0, keepdims=True).astype(jnp.int32)
        placed_ref[...] = owner * capacity + ranking

    position = placed_ref[...]
    position_ref[...] = position
    first = pl.program_id(0) * block_slots
    placing = (
        lax.broadcasted_iota(jnp.int32, (block_slots, cand_rows), 0) + first == position
    ).astype(jnp.bfloat16)
    packed_ref[...] = jnp.dot(
        placing, emb_ref[...], preferred_element_type=jnp.float32
    ).astype(packed_ref.dtype)


def pack_rows(cand_emb, cand_route, user_count, group_size):
    cand_rows, features = cand_emb.shape
    slots = 2 * cand_rows
    block_slots = slots // 2
    return pl.pallas_call(
        functools.partial(pack_kernel, group_size=group_size, user_count=user_count),
        grid=(slots // block_slots,),
        out_shape=(
            jax.ShapeDtypeStruct((slots, features), jnp.bfloat16),
            jax.ShapeDtypeStruct((1, cand_rows), jnp.int32),
        ),
        in_specs=[
            pl.BlockSpec((1, cand_rows), lambda i: (0, 0)),
            pl.BlockSpec((cand_rows, features), lambda i: (0, 0)),
        ],
        out_specs=(
            pl.BlockSpec((block_slots, features), lambda i: (i, 0)),
            pl.BlockSpec((1, cand_rows), lambda i: (0, 0)),
        ),
        scratch_shapes=[pltpu.VMEM((1, cand_rows), jnp.int32)],
        compiler_params=pltpu.CompilerParams(dimension_semantics=("arbitrary",)),
        cost_estimate=pl.CostEstimate(
            flops=2 * slots * cand_rows * features + 2 * user_count * cand_rows * cand_rows,
            transcendentals=0,
            bytes_accessed=2 * (cand_emb.size + slots * features),
        ),
    )(cand_route.reshape(1, cand_rows), cand_emb)


def local(cand_emb, cand_route, hist_kv, hist_len, w_in, w_out):
    cand_rows, features = cand_emb.shape
    user_count = lax.axis_size("user")
    group_size = lax.axis_size("cand")
    packed, position = pack_rows(cand_emb, cand_route, user_count, group_size)
    slots = packed.shape[0]
    capacity = slots // user_count
    placing = (lax.broadcasted_iota(jnp.int32, (slots, cand_rows), 0) == position).astype(
        jnp.bfloat16
    )
    outgoing = packed.reshape(user_count, capacity, features)
    items = lax.all_to_all(outgoing, "user", split_axis=0, concat_axis=0, tiled=True)
    history = hist_kv.reshape(hist_kv.shape[0], hist_kv.shape[2], hist_kv.shape[3])
    delta = run_layers(items, history, hist_len, w_in, w_out)
    returned = lax.all_to_all(delta, "user", split_axis=0, concat_axis=0, tiled=True)
    gathered = lax.dot_general(
        placing,
        returned.reshape(-1, features),
        (((0,), (0,)), ((), ())),
        preferred_element_type=jnp.float32,
    )
    return cand_emb.astype(jnp.float32) + gathered


def solution(mesh):
    placed = (
        P(("user", "cand"), None),
        P(("user", "cand")),
        P(None, "user", None, None),
        P("user"),
        P(),
        P(),
    )
    return jax.shard_map(
        local, mesh=mesh, in_specs=placed, out_specs=P(("user", "cand"), None), check_vma=False
    )
```

```python
import functools

import jax
import jax.numpy as jnp
from jax import lax
from jax.experimental import pallas as pl
from jax.experimental.pallas import tpu as pltpu
from jax.sharding import PartitionSpec as P

HEADS = 4
SLOT_BLOCK = 16

epsilon = 1e-05


def silu(v):
    return v * jax.nn.sigmoid(v)


def layer_normed(values):
    center = values - jnp.mean(values, axis=-1, keepdims=True)
    spread = jnp.mean(center * center, axis=-1, keepdims=True)
    return center * lax.rsqrt(spread + epsilon)


def layers_kernel(rows_ref, w_in_ref, tables_hbm, out_ref, tables_ref, copy_sems):
    sources, slots, features = rows_ref.shape
    block_rows = sources * slots
    layer_count = w_in_ref.shape[0]
    history_span = (tables_ref.shape[1] - features) // 2
    head_dim = features // HEADS
    factor = head_dim ** (-0.5)
    step = pl.program_id(0)
    copies = [
        pltpu.make_async_copy(tables_hbm.at[layer], tables_ref.at[layer], copy_sems.at[layer])
        for layer in range(layer_count)
    ]

    @pl.when(step == 0)
    def _():
        for copy in copies:
            copy.start()

    def arrive(index):
        @pl.when(step == 0)
        def _():
            copies[index].wait()

    busy = jnp.max(jnp.abs(rows_ref[...].astype(jnp.float32))) > 0

    @pl.when(jnp.logical_not(busy))
    def _():
        out_ref[...] = jnp.zeros(out_ref.shape, out_ref.dtype)
        for index in range(len(copies)):
            arrive(index)

    @pl.when(busy)
    def _():
        start = rows_ref[...].astype(jnp.float32).reshape(block_rows, features)
        residual = start
        for layer_index in range(layer_count):
            normed = layer_normed(residual).astype(jnp.bfloat16)
            mixed = jnp.dot(normed, w_in_ref[layer_index], preferred_element_type=jnp.float32)
            projected = silu(mixed).astype(jnp.bfloat16)
            gate = projected[:, :features].astype(jnp.float32)
            arrive(layer_index)
            heads = []
            for head in range(HEADS):
                low = head * head_dim
                query = projected[:, features + low:features + low + head_dim]
                keys = tables_ref[layer_index, :history_span, low:low + head_dim]
                values = tables_ref[
                    layer_index, history_span:2 * history_span, low:low + head_dim
                ]
                scores = lax.dot_general(
                    query, keys, (((1,), (1,)), ((), ())), preferred_element_type=jnp.float32
                )
                weight = silu(scores * factor).astype(jnp.bfloat16)
                heads.append(
                    jnp.dot(
                        weight,
                        values,
                        preferred_element_type=jnp.float32,
                    )
                )
            attended = jnp.concatenate(heads, axis=1)
            branch = (layer_normed(attended) * gate).astype(jnp.bfloat16)
            residual = residual + jnp.dot(
                branch,
                tables_ref[layer_index, 2 * history_span:, :],
                preferred_element_type=jnp.float32,
            )
        out_ref[...] = (residual - start).reshape(sources, slots, features).astype(out_ref.dtype)


def run_layers(buckets, history, length, w_in, w_out):
    sources, capacity, features = buckets.shape
    layer_count, history_span, width = history.shape
    in_history = lax.broadcasted_iota(jnp.int32, (1, history_span, 1), 1) < length[0]
    tables = jnp.concatenate(
        [
            history[:, :, :features],
            jnp.where(in_history, history[:, :, features:], jnp.zeros((), history.dtype)),
            w_out,
        ],
        axis=1,
    )
    steps = capacity // SLOT_BLOCK
    grid_spec = pltpu.PrefetchScalarGridSpec(
        num_scalar_prefetch=0,
        grid=(steps,),
        in_specs=[
            pl.BlockSpec((sources, SLOT_BLOCK, features), lambda i: (0, i, 0)),
            pl.BlockSpec(w_in.shape, lambda i: (0, 0, 0)),
            pl.BlockSpec(memory_space=pltpu.MemorySpace.HBM),
        ],
        out_specs=pl.BlockSpec((sources, SLOT_BLOCK, features), lambda i: (0, i, 0)),
        scratch_shapes=[
            pltpu.VMEM(tables.shape, tables.dtype),
            pltpu.SemaphoreType.DMA((layer_count,)),
        ],
    )
    row_count = sources * capacity
    flops = 2 * row_count * layer_count * (
        features * 2 * features + 2 * history_span * features + features * features
    )
    return pl.pallas_call(
        layers_kernel,
        grid_spec=grid_spec,
        out_shape=jax.ShapeDtypeStruct(buckets.shape, jnp.bfloat16),
        compiler_params=pltpu.CompilerParams(
            dimension_semantics=("arbitrary",), vmem_limit_bytes=48 * 1024 * 1024
        ),
        cost_estimate=pl.CostEstimate(
            flops=flops,
            transcendentals=row_count * layer_count * (HEADS * history_span + 2 * features),
            bytes_accessed=2 * (history.size + w_in.size + w_out.size + 2 * buckets.size),
        ),
    )(buckets, w_in, tables)


def pack_kernel(route_ref, column_ref, emb_ref, packed_ref, position_ref, *, group_size, user_count):
    cand_rows = emb_ref.shape[0]
    capacity = packed_ref.shape[0] // user_count
    owner = route_ref[...] // group_size
    member = (lax.broadcasted_iota(jnp.int32, (user_count, cand_rows), 0) == owner).astype(
        jnp.float32
    )
    earlier = (
        lax.broadcasted_iota(jnp.int32, (cand_rows, cand_rows), 0)
        < lax.broadcasted_iota(jnp.int32, (cand_rows, cand_rows), 1)
    ).astype(jnp.bfloat16)
    before = jnp.dot(member.astype(jnp.bfloat16), earlier, preferred_element_type=jnp.float32)
    ranking = jnp.sum(member * before, axis=0, keepdims=True).astype(jnp.int32)
    position = owner * capacity + ranking
    owner_column = column_ref[...] // group_size
    member_column = (
        lax.broadcasted_iota(jnp.int32, (cand_rows, user_count), 1) == owner_column
    ).astype(jnp.float32)
    later = (
        lax.broadcasted_iota(jnp.int32, (cand_rows, cand_rows), 1)
        < lax.broadcasted_iota(jnp.int32, (cand_rows, cand_rows), 0)
    ).astype(jnp.bfloat16)
    before_column = jnp.dot(
        later, member_column.astype(jnp.bfloat16), preferred_element_type=jnp.float32
    )
    ranking_column = jnp.sum(member_column * before_column, axis=1, keepdims=True)
    position_ref[...] = owner_column * capacity + ranking_column.astype(jnp.int32)
    placing = (
        lax.broadcasted_iota(jnp.int32, (packed_ref.shape[0], cand_rows), 0) == position
    ).astype(jnp.bfloat16)
    packed_ref[...] = jnp.dot(
        placing, emb_ref[...], preferred_element_type=jnp.float32
    ).astype(packed_ref.dtype)


def pack_rows(cand_emb, cand_route, user_count, group_size):
    cand_rows, features = cand_emb.shape
    slots = 2 * cand_rows
    return pl.pallas_call(
        functools.partial(pack_kernel, group_size=group_size, user_count=user_count),
        out_shape=(
            jax.ShapeDtypeStruct((slots, features), jnp.bfloat16),
            jax.ShapeDtypeStruct((cand_rows, 1), jnp.int32),
        ),
        in_specs=[pl.BlockSpec(memory_space=pltpu.VMEM)] * 3,
        out_specs=(pl.BlockSpec(memory_space=pltpu.VMEM),) * 2,
        cost_estimate=pl.CostEstimate(
            flops=2 * slots * cand_rows * features + 4 * user_count * cand_rows * cand_rows,
            transcendentals=0,
            bytes_accessed=2 * (cand_emb.size + slots * features),
        ),
    )(cand_route.reshape(1, cand_rows), cand_route.reshape(cand_rows, 1), cand_emb)


def unpack_kernel(returned_ref, position_ref, emb_ref, out_ref):
    cand_rows, slots = position_ref.shape[0], returned_ref.shape[0]
    picking = (
        lax.broadcasted_iota(jnp.int32, (cand_rows, slots), 1) == position_ref[...]
    ).astype(jnp.bfloat16)
    out_ref[...] = emb_ref[...].astype(jnp.float32) + jnp.dot(
        picking, returned_ref[...], preferred_element_type=jnp.float32
    )


def unpack_rows(returned, position, cand_emb):
    cand_rows, features = cand_emb.shape
    return pl.pallas_call(
        unpack_kernel,
        out_shape=jax.ShapeDtypeStruct((cand_rows, features), jnp.float32),
        in_specs=[pl.BlockSpec(memory_space=pltpu.VMEM)] * 3,
        out_specs=pl.BlockSpec(memory_space=pltpu.VMEM),
        cost_estimate=pl.CostEstimate(
            flops=2 * cand_rows * returned.shape[0] * features,
            transcendentals=0,
            bytes_accessed=2 * returned.size + 6 * cand_emb.size,
        ),
    )(returned, position, cand_emb)


def local(cand_emb, cand_route, hist_kv, hist_len, w_in, w_out):
    cand_rows, features = cand_emb.shape
    user_count = lax.axis_size("user")
    group_size = lax.axis_size("cand")
    packed, position = pack_rows(cand_emb, cand_route, user_count, group_size)
    slots = packed.shape[0]
    capacity = slots // user_count
    outgoing = packed.reshape(user_count, capacity, features)
    items = lax.all_to_all(outgoing, "user", split_axis=0, concat_axis=0, tiled=True)
    history = hist_kv.reshape(hist_kv.shape[0], hist_kv.shape[2], hist_kv.shape[3])
    delta = run_layers(items, history, hist_len, w_in, w_out)
    returned = lax.all_to_all(delta, "user", split_axis=0, concat_axis=0, tiled=True)
    return unpack_rows(returned.reshape(-1, features), position, cand_emb)


def solution(mesh):
    placed = (
        P(("user", "cand"), None),
        P(("user", "cand")),
        P(None, "user", None, None),
        P("user"),
        P(),
        P(),
    )
    return jax.shard_map(
        local, mesh=mesh, in_specs=placed, out_specs=P(("user", "cand"), None), check_vma=False
    )
```

```python
import functools

import jax
import jax.numpy as jnp
from jax import lax
from jax.experimental import pallas as pl
from jax.experimental.pallas import tpu as pltpu
from jax.sharding import PartitionSpec as P

HEADS = 4
SLOT_BLOCK = 16

epsilon = 1e-05


def silu(v):
    return v * jax.nn.sigmoid(v)


def layer_normed(values):
    center = values - jnp.mean(values, axis=-1, keepdims=True)
    spread = jnp.mean(center * center, axis=-1, keepdims=True)
    return center * lax.rsqrt(spread + epsilon)


def layers_kernel(rows_ref, w_in_ref, tables_hbm, out_ref, tables_ref, copy_sems):
    sources, slots, features = rows_ref.shape
    block_rows = sources * slots
    layer_count = w_in_ref.shape[0]
    history_span = (tables_ref.shape[1] - features) // 2
    head_dim = features // HEADS
    factor = head_dim ** (-0.5)
    step = pl.program_id(0)
    copies = [
        pltpu.make_async_copy(tables_hbm.at[layer], tables_ref.at[layer], copy_sems.at[layer])
        for layer in range(layer_count)
    ]

    @pl.when(step == 0)
    def _():
        for copy in copies:
            copy.start()

    def arrive(index):
        @pl.when(step == 0)
        def _():
            copies[index].wait()

    busy = jnp.max(jnp.abs(rows_ref[...].astype(jnp.float32))) > 0

    @pl.when(jnp.logical_not(busy))
    def _():
        out_ref[...] = jnp.zeros(out_ref.shape, out_ref.dtype)
        for index in range(len(copies)):
            arrive(index)

    @pl.when(busy)
    def _():
        start = rows_ref[...].astype(jnp.float32).reshape(block_rows, features)
        residual = start
        for layer_index in range(layer_count):
            normed = layer_normed(residual).astype(jnp.bfloat16)
            mixed = jnp.dot(normed, w_in_ref[layer_index], preferred_element_type=jnp.float32)
            projected = silu(mixed).astype(jnp.bfloat16)
            gate = projected[:, :features].astype(jnp.float32)
            arrive(layer_index)
            heads = []
            for head in range(HEADS):
                low = head * head_dim
                query = projected[:, features + low:features + low + head_dim]
                keys = tables_ref[layer_index, :history_span, low:low + head_dim]
                values = tables_ref[
                    layer_index, history_span:2 * history_span, low:low + head_dim
                ]
                scores = lax.dot_general(
                    query, keys, (((1,), (1,)), ((), ())), preferred_element_type=jnp.float32
                )
                weight = silu(scores * factor).astype(jnp.bfloat16)
                heads.append(
                    jnp.dot(
                        weight,
                        values,
                        preferred_element_type=jnp.float32,
                    )
                )
            attended = jnp.concatenate(heads, axis=1)
            branch = (layer_normed(attended) * gate).astype(jnp.bfloat16)
            residual = residual + jnp.dot(
                branch,
                tables_ref[layer_index, 2 * history_span:, :],
                preferred_element_type=jnp.float32,
            )
        out_ref[...] = (residual - start).reshape(sources, slots, features).astype(out_ref.dtype)


def run_layers(buckets, history, length, w_in, w_out):
    sources, capacity, features = buckets.shape
    layer_count, history_span, width = history.shape
    in_history = lax.broadcasted_iota(jnp.int32, (1, history_span, 1), 1) < length[0]
    tables = jnp.concatenate(
        [
            history[:, :, :features],
            jnp.where(in_history, history[:, :, features:], jnp.zeros((), history.dtype)),
            w_out,
        ],
        axis=1,
    )
    steps = capacity // SLOT_BLOCK
    grid_spec = pltpu.PrefetchScalarGridSpec(
        num_scalar_prefetch=0,
        grid=(steps,),
        in_specs=[
            pl.BlockSpec((sources, SLOT_BLOCK, features), lambda i: (0, i, 0)),
            pl.BlockSpec(memory_space=pltpu.VMEM),
            pl.BlockSpec(memory_space=pltpu.MemorySpace.HBM),
        ],
        out_specs=pl.BlockSpec((sources, SLOT_BLOCK, features), lambda i: (0, i, 0)),
        scratch_shapes=[
            pltpu.VMEM(tables.shape, tables.dtype),
            pltpu.SemaphoreType.DMA((layer_count,)),
        ],
    )
    row_count = sources * capacity
    flops = 2 * row_count * layer_count * (
        features * 2 * features + 2 * history_span * features + features * features
    )
    return pl.pallas_call(
        layers_kernel,
        grid_spec=grid_spec,
        out_shape=jax.ShapeDtypeStruct(buckets.shape, jnp.bfloat16),
        compiler_params=pltpu.CompilerParams(
            dimension_semantics=("arbitrary",), vmem_limit_bytes=48 * 1024 * 1024
        ),
        cost_estimate=pl.CostEstimate(
            flops=flops,
            transcendentals=row_count * layer_count * (HEADS * history_span + 2 * features),
            bytes_accessed=2 * (history.size + w_in.size + w_out.size + 2 * buckets.size),
        ),
    )(buckets, w_in, tables)


def pack_kernel(route_ref, emb_ref, packed_ref, position_ref, *, group_size, user_count):
    cand_rows = emb_ref.shape[0]
    capacity = packed_ref.shape[0] // user_count
    owner = route_ref[...] // group_size
    member = (lax.broadcasted_iota(jnp.int32, (user_count, cand_rows), 0) == owner).astype(
        jnp.float32
    )
    earlier = (
        lax.broadcasted_iota(jnp.int32, (cand_rows, cand_rows), 0)
        < lax.broadcasted_iota(jnp.int32, (cand_rows, cand_rows), 1)
    ).astype(jnp.bfloat16)
    before = jnp.dot(member.astype(jnp.bfloat16), earlier, preferred_element_type=jnp.float32)
    ranking = jnp.sum(member * before, axis=0, keepdims=True).astype(jnp.int32)
    position = owner * capacity + ranking
    position_ref[...] = position
    placing = (
        lax.broadcasted_iota(jnp.int32, (packed_ref.shape[0], cand_rows), 0) == position
    ).astype(jnp.bfloat16)
    packed_ref[...] = jnp.dot(
        placing, emb_ref[...], preferred_element_type=jnp.float32
    ).astype(packed_ref.dtype)


def pack_rows(cand_emb, cand_route, user_count, group_size):
    cand_rows, features = cand_emb.shape
    slots = 2 * cand_rows
    return pl.pallas_call(
        functools.partial(pack_kernel, group_size=group_size, user_count=user_count),
        out_shape=(
            jax.ShapeDtypeStruct((slots, features), jnp.bfloat16),
            jax.ShapeDtypeStruct((1, cand_rows), jnp.int32),
        ),
        in_specs=[pl.BlockSpec(memory_space=pltpu.VMEM)] * 2,
        out_specs=(pl.BlockSpec(memory_space=pltpu.VMEM),) * 2,
        cost_estimate=pl.CostEstimate(
            flops=2 * slots * cand_rows * features + 2 * user_count * cand_rows * cand_rows,
            transcendentals=0,
            bytes_accessed=2 * (cand_emb.size + slots * features),
        ),
    )(cand_route.reshape(1, cand_rows), cand_emb)


def local(cand_emb, cand_route, hist_kv, hist_len, w_in, w_out):
    cand_rows, features = cand_emb.shape
    user_count = lax.axis_size("user")
    group_size = lax.axis_size("cand")
    packed, position = pack_rows(cand_emb, cand_route, user_count, group_size)
    slots = packed.shape[0]
    capacity = slots // user_count
    placing = (lax.broadcasted_iota(jnp.int32, (slots, cand_rows), 0) == position).astype(
        jnp.bfloat16
    )
    outgoing = packed.reshape(user_count, capacity, features)
    items = lax.all_to_all(outgoing, "user", split_axis=0, concat_axis=0, tiled=True)
    history = hist_kv.reshape(hist_kv.shape[0], hist_kv.shape[2], hist_kv.shape[3])
    delta = run_layers(items, history, hist_len, w_in, w_out)
    returned = lax.all_to_all(delta, "user", split_axis=0, concat_axis=0, tiled=True)
    gathered = lax.dot_general(
        placing,
        returned.reshape(-1, features),
        (((0,), (0,)), ((), ())),
        preferred_element_type=jnp.float32,
    )
    return cand_emb.astype(jnp.float32) + gathered


def solution(mesh):
    placed = (
        P(("user", "cand"), None),
        P(("user", "cand")),
        P(None, "user", None, None),
        P("user"),
        P(),
        P(),
    )
    return jax.shard_map(
        local, mesh=mesh, in_specs=placed, out_specs=P(("user", "cand"), None), check_vma=False
    )
```

```python
import functools

import jax
import jax.numpy as jnp
from jax import lax
from jax.experimental import pallas as pl
from jax.experimental.pallas import tpu as pltpu
from jax.sharding import PartitionSpec as P

HEADS = 4
SLOT_BLOCK = 16

epsilon = 1e-05


def silu(v):
    return v * jax.nn.sigmoid(v)


def layer_normed(values):
    center = values - jnp.mean(values, axis=-1, keepdims=True)
    spread = jnp.mean(center * center, axis=-1, keepdims=True)
    return center * lax.rsqrt(spread + epsilon)


def layers_kernel(
    length_ref, rows_ref, w_in_ref, tables_hbm, out_ref, tables_ref, attended_ref, copy_sems
):
    sources, slots, features = rows_ref.shape
    block_rows = sources * slots
    layer_count = w_in_ref.shape[0]
    history_span = (tables_ref.shape[1] - features) // 2
    head_dim = features // HEADS
    factor = head_dim ** (-0.5)
    step = pl.program_id(0)
    copies = [
        pltpu.make_async_copy(tables_hbm.at[layer], tables_ref.at[layer], copy_sems.at[layer])
        for layer in range(layer_count)
    ]

    @pl.when(step == 0)
    def _():
        for copy in copies:
            copy.start()

    def arrive(index):
        @pl.when(step == 0)
        def _():
            copies[index].wait()

    busy = jnp.max(jnp.abs(rows_ref[...].astype(jnp.float32))) > 0

    @pl.when(jnp.logical_not(busy))
    def _():
        out_ref[...] = jnp.zeros(out_ref.shape, out_ref.dtype)
        for index in range(len(copies)):
            arrive(index)

    @pl.when(busy)
    def _():
        start = rows_ref[...].astype(jnp.float32).reshape(block_rows, features)
        residual = start
        for layer_index in range(layer_count):
            normed = layer_normed(residual).astype(jnp.bfloat16)
            mixed = jnp.dot(normed, w_in_ref[layer_index], preferred_element_type=jnp.float32)
            projected = silu(mixed).astype(jnp.bfloat16)
            gate = projected[:, :features].astype(jnp.float32)
            arrive(layer_index)
            def attend(span, layer_index=layer_index, projected=projected):
                heads = []
                for head in range(HEADS):
                    low = head * head_dim
                    query = projected[:, features + low:features + low + head_dim]
                    keys = tables_ref[layer_index, :span, low:low + head_dim]
                    values = tables_ref[
                        layer_index, history_span:history_span + span, low:low + head_dim
                    ]
                    scores = lax.dot_general(
                        query, keys, (((1,), (1,)), ((), ())), preferred_element_type=jnp.float32
                    )
                    weight = silu(scores * factor).astype(jnp.bfloat16)
                    heads.append(jnp.dot(weight, values, preferred_element_type=jnp.float32))
                attended_ref[...] = jnp.concatenate(heads, axis=1)

            short = length_ref[0] <= history_span // 2

            @pl.when(short)
            def _():
                attend(history_span // 2)

            @pl.when(jnp.logical_not(short))
            def _():
                attend(history_span)

            attended = attended_ref[...]
            branch = (layer_normed(attended) * gate).astype(jnp.bfloat16)
            residual = residual + jnp.dot(
                branch,
                tables_ref[layer_index, 2 * history_span:, :],
                preferred_element_type=jnp.float32,
            )
        out_ref[...] = (residual - start).reshape(sources, slots, features).astype(out_ref.dtype)


def run_layers(buckets, history, length, w_in, w_out):
    sources, capacity, features = buckets.shape
    layer_count, history_span, width = history.shape
    in_history = lax.broadcasted_iota(jnp.int32, (1, history_span, 1), 1) < length[0]
    tables = jnp.concatenate(
        [
            history[:, :, :features],
            jnp.where(in_history, history[:, :, features:], jnp.zeros((), history.dtype)),
            w_out,
        ],
        axis=1,
    )
    steps = capacity // SLOT_BLOCK
    grid_spec = pltpu.PrefetchScalarGridSpec(
        num_scalar_prefetch=1,
        grid=(steps,),
        in_specs=[
            pl.BlockSpec((sources, SLOT_BLOCK, features), lambda i, n: (0, i, 0)),
            pl.BlockSpec(w_in.shape, lambda i, n: (0, 0, 0)),
            pl.BlockSpec(memory_space=pltpu.MemorySpace.HBM),
        ],
        out_specs=pl.BlockSpec((sources, SLOT_BLOCK, features), lambda i, n: (0, i, 0)),
        scratch_shapes=[
            pltpu.VMEM(tables.shape, tables.dtype),
            pltpu.VMEM((sources * SLOT_BLOCK, features), jnp.float32),
            pltpu.SemaphoreType.DMA((layer_count,)),
        ],
    )
    row_count = sources * capacity
    flops = 2 * row_count * layer_count * (
        features * 2 * features + 2 * history_span * features + features * features
    )
    return pl.pallas_call(
        layers_kernel,
        grid_spec=grid_spec,
        out_shape=jax.ShapeDtypeStruct(buckets.shape, jnp.bfloat16),
        compiler_params=pltpu.CompilerParams(
            dimension_semantics=("arbitrary",), vmem_limit_bytes=48 * 1024 * 1024
        ),
        cost_estimate=pl.CostEstimate(
            flops=flops,
            transcendentals=row_count * layer_count * (HEADS * history_span + 2 * features),
            bytes_accessed=2 * (history.size + w_in.size + w_out.size + 2 * buckets.size),
        ),
    )(length, buckets, w_in, tables)


def pack_kernel(route_ref, emb_ref, packed_ref, position_ref, *, group_size, user_count):
    cand_rows = emb_ref.shape[0]
    capacity = packed_ref.shape[0] // user_count
    owner = route_ref[...] // group_size
    member = (lax.broadcasted_iota(jnp.int32, (user_count, cand_rows), 0) == owner).astype(
        jnp.float32
    )
    earlier = (
        lax.broadcasted_iota(jnp.int32, (cand_rows, cand_rows), 0)
        < lax.broadcasted_iota(jnp.int32, (cand_rows, cand_rows), 1)
    ).astype(jnp.bfloat16)
    before = jnp.dot(member.astype(jnp.bfloat16), earlier, preferred_element_type=jnp.float32)
    ranking = jnp.sum(member * before, axis=0, keepdims=True).astype(jnp.int32)
    position = owner * capacity + ranking
    position_ref[...] = position
    placing = (
        lax.broadcasted_iota(jnp.int32, (packed_ref.shape[0], cand_rows), 0) == position
    ).astype(jnp.bfloat16)
    packed_ref[...] = jnp.dot(
        placing, emb_ref[...], preferred_element_type=jnp.float32
    ).astype(packed_ref.dtype)


def pack_rows(cand_emb, cand_route, user_count, group_size):
    cand_rows, features = cand_emb.shape
    slots = 2 * cand_rows
    return pl.pallas_call(
        functools.partial(pack_kernel, group_size=group_size, user_count=user_count),
        out_shape=(
            jax.ShapeDtypeStruct((slots, features), jnp.bfloat16),
            jax.ShapeDtypeStruct((1, cand_rows), jnp.int32),
        ),
        in_specs=[pl.BlockSpec(memory_space=pltpu.VMEM)] * 2,
        out_specs=(pl.BlockSpec(memory_space=pltpu.VMEM),) * 2,
        cost_estimate=pl.CostEstimate(
            flops=2 * slots * cand_rows * features + 2 * user_count * cand_rows * cand_rows,
            transcendentals=0,
            bytes_accessed=2 * (cand_emb.size + slots * features),
        ),
    )(cand_route.reshape(1, cand_rows), cand_emb)


def local(cand_emb, cand_route, hist_kv, hist_len, w_in, w_out):
    cand_rows, features = cand_emb.shape
    user_count = lax.axis_size("user")
    group_size = lax.axis_size("cand")
    packed, position = pack_rows(cand_emb, cand_route, user_count, group_size)
    slots = packed.shape[0]
    capacity = slots // user_count
    placing = (lax.broadcasted_iota(jnp.int32, (slots, cand_rows), 0) == position).astype(
        jnp.bfloat16
    )
    outgoing = packed.reshape(user_count, capacity, features)
    items = lax.all_to_all(outgoing, "user", split_axis=0, concat_axis=0, tiled=True)
    history = hist_kv.reshape(hist_kv.shape[0], hist_kv.shape[2], hist_kv.shape[3])
    delta = run_layers(items, history, hist_len, w_in, w_out)
    returned = lax.all_to_all(delta, "user", split_axis=0, concat_axis=0, tiled=True)
    gathered = lax.dot_general(
        placing,
        returned.reshape(-1, features),
        (((0,), (0,)), ((), ())),
        preferred_element_type=jnp.float32,
    )
    return cand_emb.astype(jnp.float32) + gathered


def solution(mesh):
    placed = (
        P(("user", "cand"), None),
        P(("user", "cand")),
        P(None, "user", None, None),
        P("user"),
        P(),
        P(),
    )
    return jax.shard_map(
        local, mesh=mesh, in_specs=placed, out_specs=P(("user", "cand"), None), check_vma=False
    )
```

```python
import functools

import jax
import jax.numpy as jnp
from jax import lax
from jax.experimental import pallas as pl
from jax.experimental.pallas import tpu as pltpu
from jax.sharding import PartitionSpec as P

HEADS = 4
SLOT_BLOCK = 16

epsilon = 1e-05


def silu(v):
    return v * jax.nn.sigmoid(v)


def layer_normed(values):
    center = values - jnp.mean(values, axis=-1, keepdims=True)
    spread = jnp.mean(center * center, axis=-1, keepdims=True)
    return center * lax.rsqrt(spread + epsilon)


def layers_kernel(rows_ref, w_in_ref, tables_hbm, out_ref, tables_ref, copy_sems):
    sources, slots, features = rows_ref.shape
    block_rows = sources * slots
    layer_count = w_in_ref.shape[0]
    history_span = (tables_ref.shape[1] - features) // 2
    head_dim = features // HEADS
    factor = head_dim ** (-0.5)
    step = pl.program_id(0)
    copies = [
        pltpu.make_async_copy(tables_hbm.at[layer], tables_ref.at[layer], copy_sems.at[layer])
        for layer in range(layer_count)
    ]

    @pl.when(step == 0)
    def _():
        copies[0].start()

    def arrive(index):
        @pl.when(step == 0)
        def _():
            copies[index].wait()
            if index + 1 < len(copies):
                copies[index + 1].start()

    busy = jnp.max(jnp.abs(rows_ref[...].astype(jnp.float32))) > 0

    @pl.when(jnp.logical_not(busy))
    def _():
        out_ref[...] = jnp.zeros(out_ref.shape, out_ref.dtype)
        for index in range(len(copies)):
            arrive(index)

    @pl.when(busy)
    def _():
        start = rows_ref[...].astype(jnp.float32).reshape(block_rows, features)
        residual = start
        for layer_index in range(layer_count):
            normed = layer_normed(residual).astype(jnp.bfloat16)
            mixed = jnp.dot(normed, w_in_ref[layer_index], preferred_element_type=jnp.float32)
            projected = silu(mixed).astype(jnp.bfloat16)
            gate = projected[:, :features].astype(jnp.float32)
            arrive(layer_index)
            heads = []
            for head in range(HEADS):
                low = head * head_dim
                query = projected[:, features + low:features + low + head_dim]
                keys = tables_ref[layer_index, :history_span, low:low + head_dim]
                values = tables_ref[
                    layer_index, history_span:2 * history_span, low:low + head_dim
                ]
                scores = lax.dot_general(
                    query, keys, (((1,), (1,)), ((), ())), preferred_element_type=jnp.float32
                )
                weight = silu(scores * factor).astype(jnp.bfloat16)
                heads.append(
                    jnp.dot(
                        weight,
                        values,
                        preferred_element_type=jnp.float32,
                    )
                )
            attended = jnp.concatenate(heads, axis=1)
            branch = (layer_normed(attended) * gate).astype(jnp.bfloat16)
            residual = residual + jnp.dot(
                branch,
                tables_ref[layer_index, 2 * history_span:, :],
                preferred_element_type=jnp.float32,
            )
        out_ref[...] = (residual - start).reshape(sources, slots, features).astype(out_ref.dtype)


def run_layers(buckets, history, length, w_in, w_out):
    sources, capacity, features = buckets.shape
    layer_count, history_span, width = history.shape
    in_history = lax.broadcasted_iota(jnp.int32, (1, history_span, 1), 1) < length[0]
    tables = jnp.concatenate(
        [
            history[:, :, :features],
            jnp.where(in_history, history[:, :, features:], jnp.zeros((), history.dtype)),
            w_out,
        ],
        axis=1,
    )
    steps = capacity // SLOT_BLOCK
    grid_spec = pltpu.PrefetchScalarGridSpec(
        num_scalar_prefetch=0,
        grid=(steps,),
        in_specs=[
            pl.BlockSpec((sources, SLOT_BLOCK, features), lambda i: (0, i, 0)),
            pl.BlockSpec(w_in.shape, lambda i: (0, 0, 0)),
            pl.BlockSpec(memory_space=pltpu.MemorySpace.HBM),
        ],
        out_specs=pl.BlockSpec((sources, SLOT_BLOCK, features), lambda i: (0, i, 0)),
        scratch_shapes=[
            pltpu.VMEM(tables.shape, tables.dtype),
            pltpu.SemaphoreType.DMA((layer_count,)),
        ],
    )
    row_count = sources * capacity
    flops = 2 * row_count * layer_count * (
        features * 2 * features + 2 * history_span * features + features * features
    )
    return pl.pallas_call(
        layers_kernel,
        grid_spec=grid_spec,
        out_shape=jax.ShapeDtypeStruct(buckets.shape, jnp.bfloat16),
        compiler_params=pltpu.CompilerParams(
            dimension_semantics=("arbitrary",), vmem_limit_bytes=48 * 1024 * 1024
        ),
        cost_estimate=pl.CostEstimate(
            flops=flops,
            transcendentals=row_count * layer_count * (HEADS * history_span + 2 * features),
            bytes_accessed=2 * (history.size + w_in.size + w_out.size + 2 * buckets.size),
        ),
    )(buckets, w_in, tables)


def pack_kernel(route_ref, emb_ref, packed_ref, position_ref, *, group_size, user_count):
    cand_rows = emb_ref.shape[0]
    capacity = packed_ref.shape[0] // user_count
    owner = route_ref[...] // group_size
    member = (lax.broadcasted_iota(jnp.int32, (user_count, cand_rows), 0) == owner).astype(
        jnp.float32
    )
    earlier = (
        lax.broadcasted_iota(jnp.int32, (cand_rows, cand_rows), 0)
        < lax.broadcasted_iota(jnp.int32, (cand_rows, cand_rows), 1)
    ).astype(jnp.bfloat16)
    before = jnp.dot(member.astype(jnp.bfloat16), earlier, preferred_element_type=jnp.float32)
    ranking = jnp.sum(member * before, axis=0, keepdims=True).astype(jnp.int32)
    position = owner * capacity + ranking
    position_ref[...] = position
    placing = (
        lax.broadcasted_iota(jnp.int32, (packed_ref.shape[0], cand_rows), 0) == position
    ).astype(jnp.bfloat16)
    packed_ref[...] = jnp.dot(
        placing, emb_ref[...], preferred_element_type=jnp.float32
    ).astype(packed_ref.dtype)


def pack_rows(cand_emb, cand_route, user_count, group_size):
    cand_rows, features = cand_emb.shape
    slots = 2 * cand_rows
    return pl.pallas_call(
        functools.partial(pack_kernel, group_size=group_size, user_count=user_count),
        out_shape=(
            jax.ShapeDtypeStruct((slots, features), jnp.bfloat16),
            jax.ShapeDtypeStruct((1, cand_rows), jnp.int32),
        ),
        in_specs=[pl.BlockSpec(memory_space=pltpu.VMEM)] * 2,
        out_specs=(pl.BlockSpec(memory_space=pltpu.VMEM),) * 2,
        cost_estimate=pl.CostEstimate(
            flops=2 * slots * cand_rows * features + 2 * user_count * cand_rows * cand_rows,
            transcendentals=0,
            bytes_accessed=2 * (cand_emb.size + slots * features),
        ),
    )(cand_route.reshape(1, cand_rows), cand_emb)


def local(cand_emb, cand_route, hist_kv, hist_len, w_in, w_out):
    cand_rows, features = cand_emb.shape
    user_count = lax.axis_size("user")
    group_size = lax.axis_size("cand")
    packed, position = pack_rows(cand_emb, cand_route, user_count, group_size)
    slots = packed.shape[0]
    capacity = slots // user_count
    placing = (lax.broadcasted_iota(jnp.int32, (slots, cand_rows), 0) == position).astype(
        jnp.bfloat16
    )
    outgoing = packed.reshape(user_count, capacity, features)
    items = lax.all_to_all(outgoing, "user", split_axis=0, concat_axis=0, tiled=True)
    history = hist_kv.reshape(hist_kv.shape[0], hist_kv.shape[2], hist_kv.shape[3])
    delta = run_layers(items, history, hist_len, w_in, w_out)
    returned = lax.all_to_all(delta, "user", split_axis=0, concat_axis=0, tiled=True)
    gathered = lax.dot_general(
        placing,
        returned.reshape(-1, features),
        (((0,), (0,)), ((), ())),
        preferred_element_type=jnp.float32,
    )
    return cand_emb.astype(jnp.float32) + gathered


def solution(mesh):
    placed = (
        P(("user", "cand"), None),
        P(("user", "cand")),
        P(None, "user", None, None),
        P("user"),
        P(),
        P(),
    )
    return jax.shard_map(
        local, mesh=mesh, in_specs=placed, out_specs=P(("user", "cand"), None), check_vma=False
    )
```

```python
import functools

import jax
import jax.numpy as jnp
from jax import lax
from jax.experimental import pallas as pl
from jax.experimental.pallas import tpu as pltpu
from jax.sharding import PartitionSpec as P

HEADS = 4
SLOT_BLOCK = 16

epsilon = 1e-05


def silu(v):
    return v * jax.nn.sigmoid(v)


def layer_normed(values):
    center = values - jnp.mean(values, axis=-1, keepdims=True)
    spread = jnp.mean(center * center, axis=-1, keepdims=True)
    return center * lax.rsqrt(spread + epsilon)


def layers_kernel(rows_ref, w_in_ref, tables_hbm, out_ref, tables_ref, copy_sems):
    sources, slots, features = rows_ref.shape
    block_rows = sources * slots
    layer_count = w_in_ref.shape[0]
    history_span = (tables_ref.shape[1] - features) // 2
    head_dim = features // HEADS
    factor = head_dim ** (-0.5)
    step = pl.program_id(0)
    copies = [
        pltpu.make_async_copy(tables_hbm.at[layer], tables_ref.at[layer], copy_sems.at[layer])
        for layer in range(layer_count)
    ]

    @pl.when(step == 0)
    def _():
        for copy in copies:
            copy.start()

    def arrive(index):
        @pl.when(step == 0)
        def _():
            copies[index].wait()

    busy = jnp.max(jnp.abs(rows_ref[...].astype(jnp.float32))) > 0

    @pl.when(jnp.logical_not(busy))
    def _():
        out_ref[...] = jnp.zeros(out_ref.shape, out_ref.dtype)
        for index in range(len(copies)):
            arrive(index)

    @pl.when(busy)
    def _():
        start = rows_ref[...].astype(jnp.float32).reshape(block_rows, features)
        residual = start
        for layer_index in range(layer_count):
            normed = layer_normed(residual).astype(jnp.bfloat16)
            mixed = jnp.dot(normed, w_in_ref[layer_index], preferred_element_type=jnp.float32)
            projected = silu(mixed).astype(jnp.bfloat16)
            gate = projected[:, :features].astype(jnp.float32)
            arrive(layer_index)
            heads = []
            for head in range(HEADS):
                low = head * head_dim
                query = projected[:, features + low:features + low + head_dim]
                keys = tables_ref[layer_index, :history_span, low:low + head_dim]
                values = tables_ref[
                    layer_index, history_span:2 * history_span, low:low + head_dim
                ]
                scores = lax.dot_general(
                    query, keys, (((1,), (1,)), ((), ())), preferred_element_type=jnp.float32
                )
                weight = silu(scores * factor).astype(jnp.bfloat16)
                heads.append(
                    jnp.dot(
                        weight,
                        values,
                        preferred_element_type=jnp.float32,
                    )
                )
            attended = jnp.concatenate(heads, axis=1)
            branch = (layer_normed(attended) * gate).astype(jnp.bfloat16)
            residual = residual + jnp.dot(
                branch,
                tables_ref[layer_index, 2 * history_span:, :],
                preferred_element_type=jnp.float32,
            )
        out_ref[...] = (residual - start).reshape(sources, slots, features).astype(out_ref.dtype)


def run_layers(buckets, history, length, w_in, w_out):
    sources, capacity, features = buckets.shape
    layer_count, history_span, width = history.shape
    in_history = lax.broadcasted_iota(jnp.int32, (1, history_span, 1), 1) < length[0]
    tables = jnp.concatenate(
        [
            history[:, :, :features],
            jnp.where(in_history, history[:, :, features:], jnp.zeros((), history.dtype)),
            w_out,
        ],
        axis=1,
    )
    steps = capacity // SLOT_BLOCK
    grid_spec = pltpu.PrefetchScalarGridSpec(
        num_scalar_prefetch=0,
        grid=(steps,),
        in_specs=[
            pl.BlockSpec((sources, SLOT_BLOCK, features), lambda i: (0, i, 0)),
            pl.BlockSpec(w_in.shape, lambda i: (0, 0, 0)),
            pl.BlockSpec(memory_space=pltpu.MemorySpace.HBM),
        ],
        out_specs=pl.BlockSpec((sources, SLOT_BLOCK, features), lambda i: (0, i, 0)),
        scratch_shapes=[
            pltpu.VMEM(tables.shape, tables.dtype),
            pltpu.SemaphoreType.DMA((layer_count,)),
        ],
    )
    row_count = sources * capacity
    flops = 2 * row_count * layer_count * (
        features * 2 * features + 2 * history_span * features + features * features
    )
    return pl.pallas_call(
        layers_kernel,
        grid_spec=grid_spec,
        out_shape=jax.ShapeDtypeStruct(buckets.shape, jnp.bfloat16),
        compiler_params=pltpu.CompilerParams(
            dimension_semantics=("arbitrary",), vmem_limit_bytes=48 * 1024 * 1024
        ),
        cost_estimate=pl.CostEstimate(
            flops=flops,
            transcendentals=row_count * layer_count * (HEADS * history_span + 2 * features),
            bytes_accessed=2 * (history.size + w_in.size + w_out.size + 2 * buckets.size),
        ),
    )(buckets, w_in, tables)


def pack_kernel(
    route_ref, emb_ref, packed_hbm, position_ref, staged_ref, copy_sems, *, group_size, user_count
):
    cand_rows = emb_ref.shape[0]
    parts, part_slots = staged_ref.shape[0], staged_ref.shape[1]
    capacity = parts * part_slots // user_count
    owner = route_ref[...] // group_size
    member = (lax.broadcasted_iota(jnp.int32, (user_count, cand_rows), 0) == owner).astype(
        jnp.float32
    )
    earlier = (
        lax.broadcasted_iota(jnp.int32, (cand_rows, cand_rows), 0)
        < lax.broadcasted_iota(jnp.int32, (cand_rows, cand_rows), 1)
    ).astype(jnp.bfloat16)
    before = jnp.dot(member.astype(jnp.bfloat16), earlier, preferred_element_type=jnp.float32)
    ranking = jnp.sum(member * before, axis=0, keepdims=True).astype(jnp.int32)
    position = owner * capacity + ranking
    position_ref[...] = position
    copies = []
    for part in range(parts):
        placing = (
            lax.broadcasted_iota(jnp.int32, (part_slots, cand_rows), 0) + part * part_slots
            == position
        ).astype(jnp.bfloat16)
        staged_ref[part] = jnp.dot(
            placing, emb_ref[...], preferred_element_type=jnp.float32
        ).astype(staged_ref.dtype)
        copy = pltpu.make_async_copy(
            staged_ref.at[part],
            packed_hbm.at[pl.ds(part * part_slots, part_slots)],
            copy_sems.at[part],
        )
        copy.start()
        copies.append(copy)
    for copy in copies:
        copy.wait()


def pack_rows(cand_emb, cand_route, user_count, group_size):
    cand_rows, features = cand_emb.shape
    slots = 2 * cand_rows
    parts = 2
    return pl.pallas_call(
        functools.partial(pack_kernel, group_size=group_size, user_count=user_count),
        out_shape=(
            jax.ShapeDtypeStruct((slots, features), jnp.bfloat16),
            jax.ShapeDtypeStruct((1, cand_rows), jnp.int32),
        ),
        in_specs=[pl.BlockSpec(memory_space=pltpu.VMEM)] * 2,
        out_specs=(pl.BlockSpec(memory_space=pl.ANY), pl.BlockSpec(memory_space=pltpu.VMEM)),
        scratch_shapes=[
            pltpu.VMEM((parts, slots // parts, features), jnp.bfloat16),
            pltpu.SemaphoreType.DMA((parts,)),
        ],
        cost_estimate=pl.CostEstimate(
            flops=2 * slots * cand_rows * features + 2 * user_count * cand_rows * cand_rows,
            transcendentals=0,
            bytes_accessed=2 * (cand_emb.size + slots * features),
        ),
    )(cand_route.reshape(1, cand_rows), cand_emb)


def local(cand_emb, cand_route, hist_kv, hist_len, w_in, w_out):
    cand_rows, features = cand_emb.shape
    user_count = lax.axis_size("user")
    group_size = lax.axis_size("cand")
    packed, position = pack_rows(cand_emb, cand_route, user_count, group_size)
    slots = packed.shape[0]
    capacity = slots // user_count
    placing = (lax.broadcasted_iota(jnp.int32, (slots, cand_rows), 0) == position).astype(
        jnp.bfloat16
    )
    outgoing = packed.reshape(user_count, capacity, features)
    items = lax.all_to_all(outgoing, "user", split_axis=0, concat_axis=0, tiled=True)
    history = hist_kv.reshape(hist_kv.shape[0], hist_kv.shape[2], hist_kv.shape[3])
    delta = run_layers(items, history, hist_len, w_in, w_out)
    returned = lax.all_to_all(delta, "user", split_axis=0, concat_axis=0, tiled=True)
    gathered = lax.dot_general(
        placing,
        returned.reshape(-1, features),
        (((0,), (0,)), ((), ())),
        preferred_element_type=jnp.float32,
    )
    return cand_emb.astype(jnp.float32) + gathered


def solution(mesh):
    placed = (
        P(("user", "cand"), None),
        P(("user", "cand")),
        P(None, "user", None, None),
        P("user"),
        P(),
        P(),
    )
    return jax.shard_map(
        local, mesh=mesh, in_specs=placed, out_specs=P(("user", "cand"), None), check_vma=False
    )
```
